256 devices in a mesh: group: 128 (over y, z, x), depth: 2 (over core).
Axes of the slice: x: 4, y: 4, z: 8, core: 2. Of those that a mesh axis runs over, the one named last changes fastest.
Arguments:
- fwd_now: float32 [125, 65536], P(None, ('group', 'depth')), may hold values from -6 to 6
- fwd_prev: float32 [125, 65536], P(None, ('group', 'depth')), may hold values from -6 to 6
- adj_now: float32 [125, 65536], P(None, ('group', 'depth')), may hold values from -6 to 6
- adj_prev: float32 [125, 65536], P(None, ('group', 'depth')), may hold values from -6 to 6
- speed_sq: float32 [65536], P(('group', 'depth')), may hold values from 0.5 to 2
- face_lists: int32 [6, 65536], P(None, ('group', 'depth')), may hold values from 0 to 511, as said below
- send_low: int32 [65536], P(('group', 'depth')), may hold values from 0 to 255, as said below
- send_high: int32 [65536], P(('group', 'depth')), may hold values from 0 to 255, as said below
- send_radial: int32 [4096], P(('group', 'depth')), may hold values from 0 to 255, as said below
- owner_dev: int32 [65536, 1], P(('group', 'depth')), may hold values from 0 to 255; in each aligned block of 256 rows (0 to 255, 256 to 511, ...) at most 3 rows name the same one
- param_slot: int32 [65536], P(('group', 'depth')), may hold values from 0 to 127
Outputs:
- fwd_out: float32 [125, 65536], P(None, ('group', 'depth'))
- adj_out: float32 [125, 65536], P(None, ('group', 'depth'))
- param_grad: float32 [32768, 125], P(('group', 'depth'))
The draws below stay inside these ranges and needn't reach their ends.
Inputs may be any that keep to these rules, and one draw needn't show every extreme that they name: Each device's elements form a structured block of 1 x 16 x 16 elements stored in a device-specific order; face_lists names each element's touching face in its direction's pool, or the pool's last zero entry at an outer surface or a side of the block along the second lateral direction. `send_low`: distinct elements of one device, ordered by position on the face. `send_high`: distinct elements of one device, ordered by position on the face. `send_radial`: distinct elements of one device: the top layer on depth 0, the bottom layer on depth 1. `owner_dev`: among the elements of one device, no owner is named more than 3 times.
All inputs are finite; a program needn't handle non-finite values.
Results may differ from the reference program's by a relative error of at most 0.0001.
Values sent between devices are 32-bit elements; how exact they have to be, the bound alone decides.
No kernel may reach another device: no remote copies, remote signals or barrier semaphores. Data moves between devices by JAX's collectives and lax.ppermute only.
A program may use at most 64 MiB of HBM per device.

```python
import math
import jax
import jax.numpy as jnp
import numpy as np
from jax import lax

NODES = 125
STEPS = 4
GA = 1
GB = 16
GC = 16
P_DEV = 128
E_DEV = 256
E_TOTAL = 65536
P_TOTAL = 32768
CAP = 3
N_GROUP = 128
N_DEPTH = 2


def storage_order(key):
    devices = N_GROUP * N_DEPTH
    base = jax.random.fold_in(key, 7)
    return jax.vmap(lambda i: jax.random.permutation(jax.random.fold_in(base, i), E_DEV))(jnp.arange(devices)).astype(jnp.int32)


def draw_send_low(key, part):
    order = storage_order(key)
    return order[:, jnp.arange(GB * GC)].reshape(-1).astype(jnp.int32)


def draw_send_high(key, part):
    order = storage_order(key)
    return order[:, (GA - 1) * GB * GC + jnp.arange(GB * GC)].reshape(-1).astype(jnp.int32)


def draw_send_radial(key, part):
    order = storage_order(key)
    devices = N_GROUP * N_DEPTH
    places = jnp.arange(GA * GB)
    depth_here = (jnp.arange(devices) % N_DEPTH)[:, None]
    top_layer = order[:, places * GC + GC - 1]
    bottom_layer = order[:, places * GC]
    return jnp.where(depth_here == 0, top_layer, bottom_layer).reshape(-1).astype(jnp.int32)


def draw_face_lists(key, part):
    order = storage_order(key)
    devices = N_GROUP * N_DEPTH
    logical = jnp.arange(E_DEV)
    along_a = logical // (GB * GC)
    along_b = logical // GC % GB
    along_g = logical % GC
    depth_here = (jnp.arange(devices) % N_DEPTH)[:, None]

    def moved(offset):
        return jnp.take(order, jnp.clip(logical + offset, 0, E_DEV - 1), axis=1)
    lateral_slot = E_DEV + along_b * GC + along_g
    radial_slot = E_DEV + along_a * GB + along_b
    radial_zero = E_DEV + GA * GB
    first = jnp.where(along_a > 0, moved(-GB * GC), lateral_slot)
    second = jnp.where(along_a < GA - 1, moved(GB * GC), lateral_slot)
    third = jnp.where(along_b > 0, moved(-GC), E_DEV)
    fourth = jnp.where(along_b < GB - 1, moved(GC), E_DEV)
    fifth = jnp.where(along_g > 0, moved(-1), jnp.where(depth_here == 1, radial_slot, radial_zero))
    sixth = jnp.where(along_g < GC - 1, moved(1), jnp.where(depth_here == 0, radial_slot, radial_zero))
    values = jnp.stack([jnp.broadcast_to(v, (devices, E_DEV)) for v in [first, second, third, fourth, fifth, sixth]], axis=1).astype(jnp.int32)
    device_ids = jnp.arange(devices)[:, None, None]
    direction_ids = jnp.arange(6)[None, :, None]
    placed = jnp.zeros((devices, 6, E_DEV), jnp.int32).at[device_ids, direction_ids, order[:, None, :]].set(values)
    return placed.transpose(1, 0, 2).reshape(6, devices * E_DEV).astype(jnp.int32)


def set_ends(values, stream_key, low, largest):
    extent = values.shape
    index_at = [jax.random.randint(jax.random.fold_in(stream_key, axis), (), 0, extent[axis]) for axis in range(len(extent))]
    values = values.at[tuple(index_at)].set(low)
    longest = extent.index(max(extent))
    index_at[longest] = (index_at[longest] + 1) % extent[longest]
    return values.at[tuple(index_at)].set(largest)


def block_scale(own_key, shape, cuts, smallest, high):
    def one(dim, shards_of):
        steps = jax.random.uniform(jax.random.fold_in(jax.random.fold_in(own_key, 6), dim), (shards_of,), jnp.float32, smallest / len(cuts), high / len(cuts))
        return jnp.repeat(jnp.exp(steps), shape[dim] // shards_of).reshape((-1,) + (1,) * (len(shape) - dim - 1))

    factor_of = one(*cuts[0])
    for cut in cuts[1:]:
        factor_of = factor_of * one(*cut)
    return factor_of


def assign_block(own_key, own, number, rows, amount, top, bound, lean):
    ranking = jax.random.permutation(own_key, amount)
    packed, usual = portions_of(amount, rows * top, bound, lean, True), portions_of(amount, rows * top, bound, lean, False)
    places = jnp.arange(amount)

    def named(lengths, offset_by):
        used = int((lengths > 0).sum())
        fixed = max(1, used // 4)
        passed = fixed + (places - fixed + offset_by * (used - fixed)) % max(1, amount - fixed)
        return jnp.zeros((amount,), jnp.int32).at[ranking[jnp.where(places < fixed, places, passed)]].set(jnp.asarray(lengths, jnp.int32))

    lengths = jnp.where(number % 4 == 0, named(packed, number // 4), named(usual, number - number // 4 - 1))
    mixed = jax.random.permutation(jax.random.fold_in(own, 3), amount)
    donor, taker = mixed[0:amount // 2 * 2:2], mixed[1:amount // 2 * 2:2]
    slack = jnp.minimum(lengths[donor] - 1, bound - lengths[taker]) // 2
    slack = jnp.where((donor == ranking[0]) | (taker == ranking[0]) | (lengths[taker] == 0), 0, jnp.maximum(slack, 0))
    passed = jax.random.randint(jax.random.fold_in(own, 4), (amount // 2,), 0, 1 << 20) % (slack + 1)
    lengths = lengths.at[donor].add(-passed).at[taker].add(passed)
    labels = jnp.searchsorted(jnp.cumsum(lengths), jnp.arange(rows * top), side="right").astype(jnp.int32)
    table = labels.reshape(top, rows).T
    table = table[jax.random.permutation(jax.random.fold_in(own, 1), rows)]
    offset_by = jax.random.randint(jax.random.fold_in(own, 2), (rows, 1), 0, top)
    return jnp.take_along_axis(table, (jnp.arange(top)[None, :] + offset_by) % top, axis=1)


def portions_of(number_of, total, limit, slope, full):
    weights = [(1 << 20) // math.isqrt(grade ** slope) + 1 for grade in range(1, number_of + 1)]
    largest = limit if full else min(limit, max(-(-total // number_of), total * weights[0] // sum(weights)))
    least = 1 if total - largest >= number_of - 1 else 0
    counts, rest = [largest] + [least] * (number_of - 1), total - largest - least * (number_of - 1)
    while rest > 0:
        movable = [i for i in range(1, number_of) if counts[i] < largest] or [i for i in range(1, number_of) if counts[i] < limit]
        mass, budget = sum([weights[i] for i in movable]), rest
        for i in movable:
            more = min(limit - counts[i], max(1, budget * weights[i] // mass), rest)
            counts[i] = counts[i] + more
            rest = rest - more
    return np.array(counts)


def noise(stream_key, shape, scale, limit, pieces=(), held_as=jnp.bfloat16):
    values = scale * jax.random.normal(stream_key, shape, jnp.float32)
    if pieces:
        values = values * block_scale(stream_key, shape, pieces, -0.22, 0.18)
    return jnp.clip(values, -limit, limit).astype(held_as)


def setup_inputs(seed: int = 0) -> dict:
    arg_keys = jax.random.split(jax.random.key(seed), 12)
    fwd_now = noise(arg_keys[0], (NODES, E_TOTAL), 1.0, 6.0, ((1, 256),), jnp.float32)
    fwd_prev = noise(arg_keys[1], (NODES, E_TOTAL), 1.0, 6.0, ((1, 256),), jnp.float32)
    adj_now = noise(arg_keys[2], (NODES, E_TOTAL), 1.0, 6.0, ((1, 256),), jnp.float32)
    adj_prev = noise(arg_keys[3], (NODES, E_TOTAL), 1.0, 6.0, ((1, 256),), jnp.float32)
    speed_sq = jnp.clip(jnp.exp(math.log(2.0) - 1.3862944 * jax.random.uniform(arg_keys[4], (E_TOTAL,), jnp.float32) ** block_scale(arg_keys[4], (E_TOTAL,), ((0, 256),), -0.2, 0.2)), 0.5, 2.0)
    face_lists = draw_face_lists(jax.random.fold_in(arg_keys[11], 71), 0)
    send_low = draw_send_low(jax.random.fold_in(arg_keys[11], 71), 0)
    send_high = draw_send_high(jax.random.fold_in(arg_keys[11], 71), 0)
    send_radial = draw_send_radial(jax.random.fold_in(arg_keys[11], 71), 0)
    owner_dev_keys = jax.random.split(jax.random.fold_in(arg_keys[9], 1), E_TOTAL // E_DEV)
    owner_dev_turns = jax.random.permutation(jax.random.fold_in(arg_keys[9], 3), E_TOTAL // E_DEV)
    owner_dev = jax.vmap(lambda own, number: assign_block(jax.random.fold_in(arg_keys[9], 2), own, number, E_DEV, N_GROUP * N_DEPTH, 1, CAP, 2))(owner_dev_keys, owner_dev_turns).reshape((E_TOTAL, 1))
    param_slot = set_ends(jax.random.randint(arg_keys[10], (E_TOTAL,), 0, P_DEV), jax.random.fold_in(arg_keys[10], 1), 0, P_DEV - 1).astype(jnp.int32)
    return dict(fwd_now=fwd_now, fwd_prev=fwd_prev, adj_now=adj_now, adj_prev=adj_prev, speed_sq=speed_sq, face_lists=face_lists, send_low=send_low, send_high=send_high, send_radial=send_radial, owner_dev=owner_dev, param_slot=param_slot)


PENALTY = 40.0
DT_SQUARED = 0.001
KERNEL_SCALE = 0.05

def gll_tables():
    points = np.array([-1.0, -math.sqrt(3.0 / 7.0), 0.0, math.sqrt(3.0 / 7.0), 1.0])
    weights = np.array([0.1, 49.0 / 90.0, 32.0 / 45.0, 49.0 / 90.0, 0.1])
    barycentric = np.array([np.prod([points[i] - points[m] for m in range(5) if m != i]) for i in range(5)])
    derivative = np.zeros((5, 5))
    for i in range(5):
        for j in range(5):
            if i != j:
                derivative[i, j] = barycentric[i] / (barycentric[j] * (points[i] - points[j]))
            else:
                derivative[i, j] = sum((1.0 / (points[i] - points[m]) for m in range(5) if m != i))
    return (weights, derivative)

def apply_axis(table, field, axis):
    forms = ['pi,i...->p...', 'pj,ij...->ip...', 'pk,ijk...->ijp...']
    return jnp.einsum(forms[axis], table, field, precision=lax.Precision.HIGHEST)

def face_index(direction):
    whole = slice(None)
    spots = [(0,), (4,), (whole, 0), (whole, 4), (whole, whole, 0), (whole, whole, 4)]
    return spots[direction]

def faces_of(field):
    return [field[face_index(f)].reshape((25,) + field.shape[3:]) for f in range(6)]

def weight_cube(ndim):
    weights, derivative = gll_tables()
    cube = weights.reshape(5, 1, 1) * weights.reshape(1, 5, 1) * weights.reshape(1, 1, 5)
    return jnp.asarray(cube.reshape((5, 5, 5) + (1,) * (ndim - 3)), jnp.float32)

def weight_face(ndim):
    weights, derivative = gll_tables()
    square = weights.reshape(5, 1) * weights.reshape(1, 5)
    return jnp.asarray(square.reshape((5, 5) + (1,) * (ndim - 3)), jnp.float32)

def accelerate(field, grads, coef, neighbours):
    weights, derivative = gll_tables()
    table_t = jnp.asarray(derivative.T, jnp.float32)
    cube = weight_cube(field.ndim)
    stiff = apply_axis(table_t, cube * coef * grads[0], 0)
    stiff = stiff + apply_axis(table_t, cube * coef * grads[1], 1)
    stiff = stiff + apply_axis(table_t, cube * coef * grads[2], 2)
    penal = jnp.zeros_like(field)
    wface = weight_face(field.ndim)
    for f in range(6):
        spot = face_index(f)
        own = field[spot]
        other = neighbours[f].reshape(own.shape)
        penal = penal.at[spot].add(PENALTY * wface * (own - other))
    return -(stiff + penal) / cube

def reference(fwd_now, fwd_prev, adj_now, adj_prev, speed_sq, face_lists, send_low, send_high, send_radial, owner_dev, param_slot):
    weights, derivative = gll_tables()
    table = jnp.asarray(derivative, jnp.float32)
    shape = (5, 5, 5, N_GROUP, N_DEPTH, E_DEV)
    state = jnp.stack([fwd_now.reshape(shape), adj_now.reshape(shape)], axis=3)
    previous = jnp.stack([fwd_prev.reshape(shape), adj_prev.reshape(shape)], axis=3)
    coef = speed_sq.reshape(N_GROUP, N_DEPTH, E_DEV)
    lists = face_lists.reshape(6, N_GROUP, N_DEPTH, E_DEV)
    lows = send_low.reshape(N_GROUP, N_DEPTH, -1)[None, None]
    highs = send_high.reshape(N_GROUP, N_DEPTH, -1)[None, None]
    radials = send_radial.reshape(N_GROUP, N_DEPTH, -1)[None, None]
    depth_here = jnp.arange(N_DEPTH).reshape(1, 1, 1, N_DEPTH, 1)
    kernel_sum = jnp.zeros((5, 5, 5, N_GROUP, N_DEPTH, E_DEV), jnp.float32)
    for step in range(STEPS):
        grads = [apply_axis(table, state, d) for d in range(3)]
        product = grads[0][:, :, :, 0] * grads[0][:, :, :, 1] + grads[1][:, :, :, 0] * grads[1][:, :, :, 1] + grads[2][:, :, :, 0] * grads[2][:, :, :, 1]
        kernel_sum = kernel_sum + KERNEL_SCALE * weight_cube(6) * coef * product
        faces = faces_of(state)
        from_low = jnp.roll(jnp.take_along_axis(faces[1], highs, axis=-1), 1, axis=2)
        from_high = jnp.roll(jnp.take_along_axis(faces[0], lows, axis=-1), -1, axis=2)
        sent_radial = jnp.where(depth_here == 0, jnp.take_along_axis(faces[5], radials, axis=-1), jnp.take_along_axis(faces[4], radials, axis=-1))
        from_radial = sent_radial[:, :, :, ::-1]
        halos = [from_low, from_high, None, None, from_radial, from_radial]
        zero_face = jnp.zeros((25, 2, N_GROUP, N_DEPTH, 1), jnp.float32)
        neighbours = []
        for f in range(6):
            members = [faces[f ^ 1]] + ([halos[f]] if halos[f] is not None else []) + [zero_face]
            pool = jnp.concatenate(members, axis=-1)
            neighbours.append(jnp.take_along_axis(pool, lists[f][None, None], axis=-1))
        accel = accelerate(state, grads, coef, neighbours)
        following = 2.0 * state - previous + DT_SQUARED * accel
        previous = state
        state = following
    fwd_out = state[:, :, :, 0].reshape(NODES, E_TOTAL)
    adj_out = state[:, :, :, 1].reshape(NODES, E_TOTAL)
    cells = owner_dev[:, 0] * P_DEV + param_slot
    blocks = kernel_sum.reshape(NODES, E_TOTAL).T
    param_grad = jax.ops.segment_sum(blocks, cells, num_segments=P_TOTAL)
    return (fwd_out, adj_out, param_grad)
```

```python
import math

import jax
import jax.numpy as jnp
import numpy as np
from jax import lax
from jax.sharding import PartitionSpec as P

NODES = 125
STEPS = 4
P_DEV = 128


PENALTY = 40.0
DT_SQUARED = 0.001
KERNEL_SCALE = 0.05
HIGH = lax.Precision.HIGHEST


def from_behind(block, axis, distance):
    devices = range(lax.axis_size(axis))
    route = [((i - distance) % len(devices), i) for i in devices]
    return lax.ppermute(block, axis, route)


def swapped(block, axis, apart):
    count = lax.axis_size(axis)
    route = []
    for low in range(count):
        high = low | 1 << apart
        if high != low and high < count:
            route += [(low, high), (high, low)]
    return lax.ppermute(block, axis, route)


def gll_tables():
    points = np.array([-1.0, -math.sqrt(3.0 / 7.0), 0.0, math.sqrt(3.0 / 7.0), 1.0])
    weights = np.array([0.1, 49.0 / 90.0, 32.0 / 45.0, 49.0 / 90.0, 0.1])
    barycentric = np.array(
        [np.prod([points[i] - points[m] for m in range(5) if m != i]) for i in range(5)]
    )
    derivative = np.zeros((5, 5))
    for i in range(5):
        for j in range(5):
            if i != j:
                derivative[i, j] = barycentric[i] / (barycentric[j] * (points[i] - points[j]))
            else:
                derivative[i, j] = sum((1.0 / (points[i] - points[m]) for m in range(5) if m != i))
    return (weights, derivative)


def node_tables():
    weights, derivative = gll_tables()
    single = np.eye(5)
    operators = [
        np.kron(derivative, np.kron(single, single)),
        np.kron(single, np.kron(derivative, single)),
        np.kron(single, np.kron(single, derivative)),
    ]
    cube = np.kron(weights, np.kron(weights, weights))
    digits = [(n // 25, n // 5 % 5, n % 5) for n in range(125)]
    rows = []
    for f in range(6):
        axis_pick = f // 2
        level = 0 if f % 2 == 0 else 4
        rows.append([n for n in range(125) if digits[n][axis_pick] == level])
    square = np.kron(weights, weights)
    spread = np.zeros((125, 150))
    for f in range(6):
        for a, n in enumerate(rows[f]):
            spread[n, 25 * f + a] = 1.0
    return (operators, cube, rows, square, spread)


def mm(a, b):
    return jnp.dot(a, b, precision=HIGH, preferred_element_type=jnp.float32)


def onehot(rows, index):
    return (jnp.arange(rows, dtype=jnp.int32)[:, None] == index[None, :]).astype(jnp.float32)


def halves(x, elements):
    return jnp.concatenate([x[..., :elements], x[..., elements:]], axis=-2)


def unhalves(x):
    rows = x.shape[-2] // 2
    return jnp.concatenate([x[..., :rows, :], x[..., rows:, :]], axis=-1)


def per_device(
    fwd_now,
    fwd_prev,
    adj_now,
    adj_prev,
    speed_sq,
    face_lists,
    send_low,
    send_high,
    send_radial,
    owner_dev,
    param_slot,
):
    operators, cube_np, rows, square_np, spread_np = node_tables()
    elements = fwd_now.shape[1]
    groups = lax.axis_size("group")
    layers = lax.axis_size("depth")
    devices = groups * layers
    capacity = elements // devices + elements // (2 * devices) + 2
    radial_count = send_radial.shape[0]
    state = jnp.concatenate([fwd_now, adj_now], axis=1)
    previous = jnp.concatenate([fwd_prev, adj_prev], axis=1)
    depth_here = lax.axis_index("depth")
    grad_op = jnp.asarray(np.concatenate(operators, axis=0), jnp.float32)
    stiff_op = jnp.asarray(np.concatenate([o.T for o in operators], axis=1), jnp.float32)
    select = jnp.asarray(spread_np.T, jnp.float32)
    swap_rows = np.concatenate([np.arange(25) + 25 * (f ^ 1) for f in range(6)])
    select_swapped = jnp.asarray(spread_np.T[swap_rows], jnp.float32)
    spread = jnp.asarray(spread_np, jnp.float32)
    cube = jnp.asarray(cube_np, jnp.float32).reshape(125, 1)
    square = jnp.asarray(np.concatenate([square_np, square_np]), jnp.float32).reshape(50, 1)
    speed2 = jnp.concatenate([speed_sq, speed_sq])
    coef = cube * speed2

    own_pick = jnp.stack([onehot(elements, face_lists[f]) for f in range(6)])
    halo_pick = [
        onehot(elements, face_lists[0] - elements),
        onehot(elements, face_lists[1] - elements),
        onehot(radial_count, face_lists[4] - elements),
        onehot(radial_count, face_lists[5] - elements),
    ]
    send_high_pick = onehot(elements, send_high)
    send_low_pick = onehot(elements, send_low)
    send_radial_pick = onehot(elements, send_radial)

    target = owner_dev[:, 0]
    counts = (target[:, None] == jnp.arange(devices, dtype=jnp.int32)[None, :]).astype(jnp.int32)
    before = jnp.cumsum(counts, axis=0) - counts
    position = jnp.sum(before * counts, axis=1)
    placing = target * capacity + position
    placer = onehot(devices * capacity, placing)
    labels = mm(placer, param_slot.astype(jnp.float32) + 1.0)

    kernel_sum = jnp.zeros((NODES, elements), jnp.float32)
    for step in range(STEPS):
        grads = mm(grad_op, state).reshape(3, NODES, 2 * elements)
        product = (
            grads[0][:, :elements] * grads[0][:, elements:]
            + grads[1][:, :elements] * grads[1][:, elements:]
            + grads[2][:, :elements] * grads[2][:, elements:]
        )
        kernel_sum = kernel_sum + KERNEL_SCALE * cube * speed_sq * product
        faces = halves(mm(select, state).reshape(6, 25, 2 * elements), elements)
        faces_sw = halves(mm(select_swapped, state).reshape(6, 25, 2 * elements), elements)
        from_low = from_behind(mm(faces[1], send_high_pick), "group", 1)
        from_high = from_behind(mm(faces[0], send_low_pick), "group", -1)
        radial_face = jnp.where(depth_here == 0, faces[5], faces[4])
        from_radial = swapped(mm(radial_face, send_radial_pick), "depth", 0)
        other = lax.dot_general(
            faces_sw,
            own_pick,
            (((2,), (1,)), ((0,), (0,))),
            precision=HIGH,
            preferred_element_type=jnp.float32,
        )
        halo_part = jnp.stack(
            [
                mm(from_low, halo_pick[0]),
                mm(from_high, halo_pick[1]),
                jnp.zeros_like(from_low),
                jnp.zeros_like(from_low),
                mm(from_radial, halo_pick[2]),
                mm(from_radial, halo_pick[3]),
            ]
        )
        other = other + halo_part
        jumps = PENALTY * square * (faces - other)
        penal = mm(spread, unhalves(jumps).reshape(150, 2 * elements))
        stiff = mm(stiff_op, (coef * grads).reshape(3 * NODES, 2 * elements))
        accel = -(stiff + penal) / cube
        following = 2.0 * state - previous + DT_SQUARED * accel
        previous = state
        state = following

    blocks = lax.dot_general(
        placer,
        kernel_sum,
        (((1,), (1,)), ((), ())),
        precision=HIGH,
        preferred_element_type=jnp.float32,
    )
    packed = jnp.concatenate([blocks, labels[:, None]], axis=1)
    got = lax.all_to_all(packed, ("group", "depth"), 0, 0, tiled=True)
    got_labels = got[:, NODES] - 1.0
    cell_ids = jnp.arange(P_DEV, dtype=jnp.float32)[:, None]
    selector = (got_labels[None, :] == cell_ids).astype(jnp.float32)
    param_grad = mm(selector, got[:, :NODES])
    return (state[:, :elements], state[:, elements:], param_grad)


def solution(mesh):
    return jax.shard_map(
        per_device,
        mesh=mesh,
        in_specs=(
            P(None, ("group", "depth")),
            P(None, ("group", "depth")),
            P(None, ("group", "depth")),
            P(None, ("group", "depth")),
            P(("group", "depth")),
            P(None, ("group", "depth")),
            P(("group", "depth")),
            P(("group", "depth")),
            P(("group", "depth")),
            P(("group", "depth"), None),
            P(("group", "depth")),
        ),
        out_specs=(
            P(None, ("group", "depth")),
            P(None, ("group", "depth")),
            P(("group", "depth"), None),
        ),
        check_vma=False,
    )
```

```python
import math

import jax
import jax.numpy as jnp
import numpy as np
from jax import lax
from jax.sharding import PartitionSpec as P

NODES = 125
STEPS = 4
P_DEV = 128


PENALTY = 40.0
DT_SQUARED = 0.001
KERNEL_SCALE = 0.05
HIGH = lax.Precision.HIGHEST


def from_behind(block, axis, distance):
    devices = range(lax.axis_size(axis))
    route = [((i - distance) % len(devices), i) for i in devices]
    return lax.ppermute(block, axis, route)


def swapped(block, axis, apart):
    count = lax.axis_size(axis)
    route = []
    for low in range(count):
        high = low | 1 << apart
        if high != low and high < count:
            route += [(low, high), (high, low)]
    return lax.ppermute(block, axis, route)


def gll_tables():
    points = np.array([-1.0, -math.sqrt(3.0 / 7.0), 0.0, math.sqrt(3.0 / 7.0), 1.0])
    weights = np.array([0.1, 49.0 / 90.0, 32.0 / 45.0, 49.0 / 90.0, 0.1])
    barycentric = np.array(
        [np.prod([points[i] - points[m] for m in range(5) if m != i]) for i in range(5)]
    )
    derivative = np.zeros((5, 5))
    for i in range(5):
        for j in range(5):
            if i != j:
                derivative[i, j] = barycentric[i] / (barycentric[j] * (points[i] - points[j]))
            else:
                derivative[i, j] = sum((1.0 / (points[i] - points[m]) for m in range(5) if m != i))
    return (weights, derivative)


def node_tables():
    weights, derivative = gll_tables()
    single = np.eye(5)
    operators = [
        np.kron(derivative, np.kron(single, single)),
        np.kron(single, np.kron(derivative, single)),
        np.kron(single, np.kron(single, derivative)),
    ]
    cube = np.kron(weights, np.kron(weights, weights))
    digits = [(n // 25, n // 5 % 5, n % 5) for n in range(125)]
    rows = []
    for f in range(6):
        axis_pick = f // 2
        level = 0 if f % 2 == 0 else 4
        rows.append([n for n in range(125) if digits[n][axis_pick] == level])
    square = np.kron(weights, weights)
    spread = np.zeros((125, 150))
    for f in range(6):
        for a, n in enumerate(rows[f]):
            spread[n, 25 * f + a] = 1.0
    return (operators, cube, rows, square, spread)


def mm(a, b):
    return jnp.dot(a, b, precision=HIGH, preferred_element_type=jnp.float32)


def onehot(rows, index):
    return (jnp.arange(rows, dtype=jnp.int32)[:, None] == index[None, :]).astype(jnp.float32)


def padded_tables(pad_nodes, pad_face):
    operators, cube_np, rows, square_np, spread_np = node_tables()
    grad_op = np.zeros((3 * pad_nodes, pad_nodes))
    stiff_op = np.zeros((pad_nodes, 3 * pad_nodes))
    for d in range(3):
        grad_op[d * pad_nodes : d * pad_nodes + NODES, :NODES] = operators[d]
        stiff_op[:NODES, d * pad_nodes : d * pad_nodes + NODES] = operators[d].T
    select = np.zeros((6 * pad_face, pad_nodes))
    select_swapped = np.zeros((6 * pad_face, pad_nodes))
    for f in range(6):
        for a in range(25):
            select[f * pad_face + a, rows[f][a]] = 1.0
            select_swapped[f * pad_face + a, rows[f ^ 1][a]] = 1.0
    cube = np.ones((pad_nodes, 1))
    cube[:NODES, 0] = cube_np
    square = np.zeros((pad_face, 1))
    square[:25, 0] = square_np
    return grad_op, stiff_op, select, select_swapped, cube, square


def per_device(
    fwd_now,
    fwd_prev,
    adj_now,
    adj_prev,
    speed_sq,
    face_lists,
    send_low,
    send_high,
    send_radial,
    owner_dev,
    param_slot,
):
    pad_nodes, pad_face = 128, 32
    grad_np, stiff_np, select_np, select_sw_np, cube_np, square_np = padded_tables(
        pad_nodes, pad_face
    )
    elements = fwd_now.shape[1]
    groups = lax.axis_size("group")
    layers = lax.axis_size("depth")
    devices = groups * layers
    capacity = elements // devices + elements // (2 * devices) + 2
    radial_count = send_radial.shape[0]
    extra = pad_nodes - NODES

    def padded(a, b):
        return jnp.pad(jnp.concatenate([a, b], axis=1), ((0, extra), (0, 0)))

    state = padded(fwd_now, adj_now)
    previous = padded(fwd_prev, adj_prev)
    depth_here = lax.axis_index("depth")
    grad_op = jnp.asarray(grad_np, jnp.float32)
    stiff_op = jnp.asarray(stiff_np, jnp.float32)
    select = jnp.asarray(select_np, jnp.float32)
    select_swapped = jnp.asarray(select_sw_np, jnp.float32)
    spread = jnp.asarray(select_np.T, jnp.float32)
    cube = jnp.asarray(cube_np, jnp.float32)
    square = jnp.asarray(square_np, jnp.float32)
    speed2 = jnp.concatenate([speed_sq, speed_sq])
    coef = cube * speed2

    own_pick = jnp.stack([onehot(elements, face_lists[f]) for f in range(6)])
    high_order = from_behind(send_high.astype(jnp.float32), "group", 1).astype(jnp.int32)
    low_order = from_behind(send_low.astype(jnp.float32), "group", -1).astype(jnp.int32)
    radial_order = swapped(send_radial.astype(jnp.float32), "depth", 0).astype(jnp.int32)

    def halo_pick(order, slots, lists):
        return mm(onehot(elements, order), onehot(slots, lists - elements))

    halo_low = halo_pick(high_order, elements, face_lists[0])
    halo_high = halo_pick(low_order, elements, face_lists[1])
    halo_bottom = halo_pick(radial_order, radial_count, face_lists[4])
    halo_top = halo_pick(radial_order, radial_count, face_lists[5])

    target = owner_dev[:, 0]
    counts = (target[:, None] == jnp.arange(devices, dtype=jnp.int32)[None, :]).astype(jnp.int32)
    before = jnp.cumsum(counts, axis=0) - counts
    position = jnp.sum(before * counts, axis=1)
    placing = target * capacity + position
    placer = onehot(devices * capacity, placing)
    labels = mm(placer, param_slot.astype(jnp.float32) + 1.0)

    def by_field(x, pick):
        return jnp.concatenate([mm(x[:, :elements], pick), mm(x[:, elements:], pick)], axis=1)

    def own_part(x):
        return lax.dot_general(
            x, own_pick, (((2,), (1,)), ((0,), (0,))), precision=HIGH,
            preferred_element_type=jnp.float32,
        )

    kernel_sum = jnp.zeros((pad_nodes, elements), jnp.float32)
    for step in range(STEPS):
        grads = mm(grad_op, state).reshape(3, pad_nodes, 2 * elements)
        product = (
            grads[0][:, :elements] * grads[0][:, elements:]
            + grads[1][:, :elements] * grads[1][:, elements:]
            + grads[2][:, :elements] * grads[2][:, elements:]
        )
        kernel_sum = kernel_sum + KERNEL_SCALE * cube * speed_sq * product
        faces = mm(select, state).reshape(6, pad_face, 2 * elements)
        from_low = from_behind(faces[1], "group", 1)
        from_high = from_behind(faces[0], "group", -1)
        radial_face = jnp.where(depth_here == 0, faces[5], faces[4])
        from_radial = swapped(radial_face, "depth", 0)
        faces_sw = mm(select_swapped, state).reshape(6, pad_face, 2 * elements)
        other = jnp.concatenate(
            [own_part(faces_sw[..., :elements]), own_part(faces_sw[..., elements:])], axis=2
        )
        zero = jnp.zeros_like(from_low)
        halo_part = jnp.stack(
            [
                by_field(from_low, halo_low),
                by_field(from_high, halo_high),
                zero,
                zero,
                by_field(from_radial, halo_bottom),
                by_field(from_radial, halo_top),
            ]
        )
        other = other + halo_part
        jumps = PENALTY * square * (faces - other)
        penal = mm(spread, jumps.reshape(6 * pad_face, 2 * elements))
        stiff = mm(stiff_op, (coef * grads).reshape(3 * pad_nodes, 2 * elements))
        accel = -(stiff + penal) / cube
        following = 2.0 * state - previous + DT_SQUARED * accel
        previous = state
        state = following

    blocks = lax.dot_general(
        placer,
        kernel_sum[:NODES],
        (((1,), (1,)), ((), ())),
        precision=HIGH,
        preferred_element_type=jnp.float32,
    )
    packed = jnp.concatenate([blocks, labels[:, None]], axis=1)
    got = lax.all_to_all(packed, ("group", "depth"), 0, 0, tiled=True)
    got_labels = got[:, NODES] - 1.0
    cell_ids = jnp.arange(P_DEV, dtype=jnp.float32)[:, None]
    selector = (got_labels[None, :] == cell_ids).astype(jnp.float32)
    param_grad = mm(selector, got[:, :NODES])
    return (state[:NODES, :elements], state[:NODES, elements:], param_grad)


def solution(mesh):
    return jax.shard_map(
        per_device,
        mesh=mesh,
        in_specs=(
            P(None, ("group", "depth")),
            P(None, ("group", "depth")),
            P(None, ("group", "depth")),
            P(None, ("group", "depth")),
            P(("group", "depth")),
            P(None, ("group", "depth")),
            P(("group", "depth")),
            P(("group", "depth")),
            P(("group", "depth")),
            P(("group", "depth"), None),
            P(("group", "depth")),
        ),
        out_specs=(
            P(None, ("group", "depth")),
            P(None, ("group", "depth")),
            P(("group", "depth"), None),
        ),
        check_vma=False,
    )
```

```python
import math

import jax
import jax.numpy as jnp
import numpy as np
from jax import lax
from jax.sharding import PartitionSpec as P

NODES = 125
STEPS = 4
P_DEV = 128


PENALTY = 40.0
DT_SQUARED = 0.001
KERNEL_SCALE = 0.05
HIGH = lax.Precision.HIGHEST


def from_behind(block, axis, distance):
    devices = range(lax.axis_size(axis))
    route = [((i - distance) % len(devices), i) for i in devices]
    return lax.ppermute(block, axis, route)


def swapped(block, axis, apart):
    count = lax.axis_size(axis)
    route = []
    for low in range(count):
        high = low | 1 << apart
        if high != low and high < count:
            route += [(low, high), (high, low)]
    return lax.ppermute(block, axis, route)


def gll_tables():
    points = np.array([-1.0, -math.sqrt(3.0 / 7.0), 0.0, math.sqrt(3.0 / 7.0), 1.0])
    weights = np.array([0.1, 49.0 / 90.0, 32.0 / 45.0, 49.0 / 90.0, 0.1])
    barycentric = np.array(
        [np.prod([points[i] - points[m] for m in range(5) if m != i]) for i in range(5)]
    )
    derivative = np.zeros((5, 5))
    for i in range(5):
        for j in range(5):
            if i != j:
                derivative[i, j] = barycentric[i] / (barycentric[j] * (points[i] - points[j]))
            else:
                derivative[i, j] = sum((1.0 / (points[i] - points[m]) for m in range(5) if m != i))
    return (weights, derivative)


def node_tables():
    weights, derivative = gll_tables()
    single = np.eye(5)
    operators = [
        np.kron(derivative, np.kron(single, single)),
        np.kron(single, np.kron(derivative, single)),
        np.kron(single, np.kron(single, derivative)),
    ]
    cube = np.kron(weights, np.kron(weights, weights))
    digits = [(n // 25, n // 5 % 5, n % 5) for n in range(125)]
    rows = []
    for f in range(6):
        axis_pick = f // 2
        level = 0 if f % 2 == 0 else 4
        rows.append([n for n in range(125) if digits[n][axis_pick] == level])
    square = np.kron(weights, weights)
    spread = np.zeros((125, 150))
    for f in range(6):
        for a, n in enumerate(rows[f]):
            spread[n, 25 * f + a] = 1.0
    return (operators, cube, rows, square, spread)


def mm(a, b):
    return jnp.dot(a, b, precision=HIGH, preferred_element_type=jnp.float32)


def onehot(rows, index):
    return (jnp.arange(rows, dtype=jnp.int32)[:, None] == index[None, :]).astype(jnp.float32)


def padded_tables(pad_nodes, pad_face):
    operators, cube_np, rows, square_np, spread_np = node_tables()
    grad_op = np.zeros((3 * pad_nodes, pad_nodes))
    stiff_op = np.zeros((pad_nodes, 3 * pad_nodes))
    for d in range(3):
        grad_op[d * pad_nodes : d * pad_nodes + NODES, :NODES] = operators[d]
        stiff_op[:NODES, d * pad_nodes : d * pad_nodes + NODES] = operators[d].T
    select = np.zeros((6 * pad_face, pad_nodes))
    select_swapped = np.zeros((6 * pad_face, pad_nodes))
    for f in range(6):
        for a in range(25):
            select[f * pad_face + a, rows[f][a]] = 1.0
            select_swapped[f * pad_face + a, rows[f ^ 1][a]] = 1.0
    cube = np.ones((pad_nodes, 1))
    cube[:NODES, 0] = cube_np
    square = np.zeros((pad_face, 1))
    square[:25, 0] = square_np
    return grad_op, stiff_op, select, select_swapped, cube, square


def per_device(
    fwd_now,
    fwd_prev,
    adj_now,
    adj_prev,
    speed_sq,
    face_lists,
    send_low,
    send_high,
    send_radial,
    owner_dev,
    param_slot,
):
    pad_nodes, pad_face = 128, 32
    grad_np, stiff_np, select_np, select_sw_np, cube_np, square_np = padded_tables(
        pad_nodes, pad_face
    )
    elements = fwd_now.shape[1]
    groups = lax.axis_size("group")
    layers = lax.axis_size("depth")
    devices = groups * layers
    capacity = elements // devices + elements // (2 * devices) + 2
    radial_count = send_radial.shape[0]
    extra = pad_nodes - NODES

    def padded(a, b):
        return jnp.pad(jnp.concatenate([a, b], axis=1), ((0, extra), (0, 0)))

    state = padded(fwd_now, adj_now)
    previous = padded(fwd_prev, adj_prev)
    depth_here = lax.axis_index("depth")
    grad_op = jnp.asarray(grad_np, jnp.float32)
    stiff_op = jnp.asarray(stiff_np, jnp.float32)
    select = jnp.asarray(select_np, jnp.float32)
    select_swapped = jnp.asarray(select_sw_np, jnp.float32)
    spread = jnp.asarray(select_np.T, jnp.float32)
    cube = jnp.asarray(cube_np, jnp.float32)
    square = jnp.asarray(square_np, jnp.float32)
    speed2 = jnp.concatenate([speed_sq, speed_sq])
    coef = cube * speed2

    own_pick = jnp.stack([onehot(elements, face_lists[f]) for f in range(6)])
    high_order = from_behind(send_high.astype(jnp.float32), "group", 1).astype(jnp.int32)
    low_order = from_behind(send_low.astype(jnp.float32), "group", -1).astype(jnp.int32)
    radial_order = swapped(send_radial.astype(jnp.float32), "depth", 0).astype(jnp.int32)

    def halo_pick(order, slots, lists):
        return mm(onehot(elements, order), onehot(slots, lists - elements))

    halo_low = halo_pick(high_order, elements, face_lists[0])
    halo_high = halo_pick(low_order, elements, face_lists[1])
    halo_bottom = halo_pick(radial_order, radial_count, face_lists[4])
    halo_top = halo_pick(radial_order, radial_count, face_lists[5])

    target = owner_dev[:, 0]
    counts = (target[:, None] == jnp.arange(devices, dtype=jnp.int32)[None, :]).astype(jnp.int32)
    before = jnp.cumsum(counts, axis=0) - counts
    position = jnp.sum(before * counts, axis=1)
    placing = target * capacity + position
    placer = onehot(devices * capacity, placing)
    labels = mm(placer, param_slot.astype(jnp.float32) + 1.0)

    def by_field(x, pick):
        return jnp.concatenate([mm(x[:, :elements], pick), mm(x[:, elements:], pick)], axis=1)

    def own_part(x):
        return lax.dot_general(
            x, own_pick, (((2,), (1,)), ((0,), (0,))), precision=HIGH,
            preferred_element_type=jnp.float32,
        )

    halo_pick_all = jnp.stack([halo_low, halo_high, halo_bottom, halo_top])
    halo_dirs = [0, 1, 4, 5]
    spread_halo = np.concatenate(
        [select_np.T[:, f * pad_face : (f + 1) * pad_face] for f in halo_dirs], axis=1
    )
    square_halo = np.tile(square_np[:, 0], len(halo_dirs))
    into_state_np = DT_SQUARED * (spread_halo / cube_np) * (PENALTY * square_halo)[None, :]
    into_state = jnp.asarray(into_state_np, jnp.float32)
    into_faces = jnp.asarray(select_np @ into_state_np, jnp.float32)

    def halo_field(blocks):
        out = lax.dot_general(
            jnp.stack(blocks), halo_pick_all, (((2,), (1,)), ((0,), (0,))), precision=HIGH,
            preferred_element_type=jnp.float32,
        )
        return out.reshape(len(halo_dirs) * pad_face, elements)

    faces = mm(select, state).reshape(6, pad_face, 2 * elements)
    kernel_sum = jnp.zeros((pad_nodes, elements), jnp.float32)
    for step in range(STEPS):
        from_low = from_behind(faces[1], "group", 1)
        from_high = from_behind(faces[0], "group", -1)
        radial_face = jnp.where(depth_here == 0, faces[5], faces[4])
        from_radial = swapped(radial_face, "depth", 0)
        grads = mm(grad_op, state).reshape(3, pad_nodes, 2 * elements)
        product = (
            grads[0][:, :elements] * grads[0][:, elements:]
            + grads[1][:, :elements] * grads[1][:, elements:]
            + grads[2][:, :elements] * grads[2][:, elements:]
        )
        kernel_sum = kernel_sum + KERNEL_SCALE * cube * speed_sq * product
        faces_sw = jnp.stack([faces[f ^ 1] for f in range(6)])
        other = jnp.concatenate(
            [own_part(faces_sw[..., :elements]), own_part(faces_sw[..., elements:])], axis=2
        )
        jumps = PENALTY * square * (faces - other)
        penal = mm(spread, jumps.reshape(6 * pad_face, 2 * elements))
        stiff = mm(stiff_op, (coef * grads).reshape(3 * pad_nodes, 2 * elements))
        partial = 2.0 * state - previous + DT_SQUARED * (-(stiff + penal) / cube)
        partial_faces = mm(select, partial)
        halo = jnp.concatenate(
            [
                halo_field([x[:, :elements] for x in (from_low, from_high, from_radial, from_radial)]),
                halo_field([x[:, elements:] for x in (from_low, from_high, from_radial, from_radial)]),
            ],
            axis=1,
        )
        faces = (partial_faces + mm(into_faces, halo)).reshape(6, pad_face, 2 * elements)
        previous = state
        state = partial + mm(into_state, halo)

    blocks = lax.dot_general(
        placer,
        kernel_sum[:NODES],
        (((1,), (1,)), ((), ())),
        precision=HIGH,
        preferred_element_type=jnp.float32,
    )
    packed = jnp.concatenate([blocks, labels[:, None]], axis=1)
    got = lax.all_to_all(packed, ("group", "depth"), 0, 0, tiled=True)
    got_labels = got[:, NODES] - 1.0
    cell_ids = jnp.arange(P_DEV, dtype=jnp.float32)[:, None]
    selector = (got_labels[None, :] == cell_ids).astype(jnp.float32)
    param_grad = mm(selector, got[:, :NODES])
    return (state[:NODES, :elements], state[:NODES, elements:], param_grad)


def solution(mesh):
    return jax.shard_map(
        per_device,
        mesh=mesh,
        in_specs=(
            P(None, ("group", "depth")),
            P(None, ("group", "depth")),
            P(None, ("group", "depth")),
            P(None, ("group", "depth")),
            P(("group", "depth")),
            P(None, ("group", "depth")),
            P(("group", "depth")),
            P(("group", "depth")),
            P(("group", "depth")),
            P(("group", "depth"), None),
            P(("group", "depth")),
        ),
        out_specs=(
            P(None, ("group", "depth")),
            P(None, ("group", "depth")),
            P(("group", "depth"), None),
        ),
        check_vma=False,
    )
```

```python
import math

import jax
import jax.numpy as jnp
import numpy as np
from jax import lax
from jax.sharding import PartitionSpec as P

NODES = 125
STEPS = 4
P_DEV = 128


PENALTY = 40.0
DT_SQUARED = 0.001
KERNEL_SCALE = 0.05
HIGH = lax.Precision.HIGHEST


def from_behind(block, axis, distance):
    devices = range(lax.axis_size(axis))
    route = [((i - distance) % len(devices), i) for i in devices]
    return lax.ppermute(block, axis, route)


def swapped(block, axis, apart):
    count = lax.axis_size(axis)
    route = []
    for low in range(count):
        high = low | 1 << apart
        if high != low and high < count:
            route += [(low, high), (high, low)]
    return lax.ppermute(block, axis, route)


def gll_tables():
    points = np.array([-1.0, -math.sqrt(3.0 / 7.0), 0.0, math.sqrt(3.0 / 7.0), 1.0])
    weights = np.array([0.1, 49.0 / 90.0, 32.0 / 45.0, 49.0 / 90.0, 0.1])
    barycentric = np.array(
        [np.prod([points[i] - points[m] for m in range(5) if m != i]) for i in range(5)]
    )
    derivative = np.zeros((5, 5))
    for i in range(5):
        for j in range(5):
            if i != j:
                derivative[i, j] = barycentric[i] / (barycentric[j] * (points[i] - points[j]))
            else:
                derivative[i, j] = sum((1.0 / (points[i] - points[m]) for m in range(5) if m != i))
    return (weights, derivative)


def node_tables():
    weights, derivative = gll_tables()
    single = np.eye(5)
    operators = [
        np.kron(derivative, np.kron(single, single)),
        np.kron(single, np.kron(derivative, single)),
        np.kron(single, np.kron(single, derivative)),
    ]
    cube = np.kron(weights, np.kron(weights, weights))
    digits = [(n // 25, n // 5 % 5, n % 5) for n in range(125)]
    rows = []
    for f in range(6):
        axis_pick = f // 2
        level = 0 if f % 2 == 0 else 4
        rows.append([n for n in range(125) if digits[n][axis_pick] == level])
    square = np.kron(weights, weights)
    spread = np.zeros((125, 150))
    for f in range(6):
        for a, n in enumerate(rows[f]):
            spread[n, 25 * f + a] = 1.0
    return (operators, cube, rows, square, spread)


def mm(a, b):
    return jnp.dot(a, b, precision=HIGH, preferred_element_type=jnp.float32)


def onehot(rows, index):
    return (jnp.arange(rows, dtype=jnp.int32)[:, None] == index[None, :]).astype(jnp.float32)


def padded_tables(pad_nodes, pad_face):
    operators, cube_np, rows, square_np, spread_np = node_tables()
    grad_op = np.zeros((3 * pad_nodes, pad_nodes))
    stiff_op = np.zeros((pad_nodes, 3 * pad_nodes))
    for d in range(3):
        grad_op[d * pad_nodes : d * pad_nodes + NODES, :NODES] = operators[d]
        stiff_op[:NODES, d * pad_nodes : d * pad_nodes + NODES] = operators[d].T
    select = np.zeros((6 * pad_face, pad_nodes))
    select_swapped = np.zeros((6 * pad_face, pad_nodes))
    for f in range(6):
        for a in range(25):
            select[f * pad_face + a, rows[f][a]] = 1.0
            select_swapped[f * pad_face + a, rows[f ^ 1][a]] = 1.0
    cube = np.ones((pad_nodes, 1))
    cube[:NODES, 0] = cube_np
    square = np.zeros((pad_face, 1))
    square[:25, 0] = square_np
    return grad_op, stiff_op, select, select_swapped, cube, square


def per_device(
    fwd_now,
    fwd_prev,
    adj_now,
    adj_prev,
    speed_sq,
    face_lists,
    send_low,
    send_high,
    send_radial,
    owner_dev,
    param_slot,
):
    pad_nodes, pad_face = 128, 32
    grad_np, stiff_np, select_np, select_sw_np, cube_np, square_np = padded_tables(
        pad_nodes, pad_face
    )
    elements = fwd_now.shape[1]
    groups = lax.axis_size("group")
    layers = lax.axis_size("depth")
    devices = groups * layers
    capacity = elements // devices + elements // (2 * devices) + 2
    radial_count = send_radial.shape[0]
    extra = pad_nodes - NODES

    def padded(a, b):
        return jnp.pad(jnp.concatenate([a, b], axis=1), ((0, extra), (0, 0)))

    state = padded(fwd_now, adj_now)
    previous = padded(fwd_prev, adj_prev)
    depth_here = lax.axis_index("depth")
    grad_op = jnp.asarray(grad_np, jnp.float32)
    stiff_op = jnp.asarray(stiff_np, jnp.float32)
    select = jnp.asarray(select_np, jnp.float32)
    select_swapped = jnp.asarray(select_sw_np, jnp.float32)
    spread = jnp.asarray(select_np.T, jnp.float32)
    cube = jnp.asarray(cube_np, jnp.float32)
    square = jnp.asarray(square_np, jnp.float32)
    speed2 = jnp.concatenate([speed_sq, speed_sq])
    coef = cube * speed2

    own_pick = jnp.stack([onehot(elements, face_lists[f]) for f in range(6)])
    high_order = from_behind(send_high.astype(jnp.float32), "group", 1).astype(jnp.int32)
    low_order = from_behind(send_low.astype(jnp.float32), "group", -1).astype(jnp.int32)
    radial_order = swapped(send_radial.astype(jnp.float32), "depth", 0).astype(jnp.int32)

    def halo_pick(order, slots, lists):
        return mm(onehot(elements, order), onehot(slots, lists - elements))

    halo_low = halo_pick(high_order, elements, face_lists[0])
    halo_high = halo_pick(low_order, elements, face_lists[1])
    halo_bottom = halo_pick(radial_order, radial_count, face_lists[4])
    halo_top = halo_pick(radial_order, radial_count, face_lists[5])

    target = owner_dev[:, 0]
    counts = (target[:, None] == jnp.arange(devices, dtype=jnp.int32)[None, :]).astype(jnp.int32)
    before = jnp.cumsum(counts, axis=0) - counts
    position = jnp.sum(before * counts, axis=1)
    placing = target * capacity + position
    placer = onehot(devices * capacity, placing)
    labels = mm(placer, param_slot.astype(jnp.float32) + 1.0)

    def by_field(x, pick):
        return jnp.concatenate([mm(x[:, :elements], pick), mm(x[:, elements:], pick)], axis=1)

    def own_part(x):
        return lax.dot_general(
            x, own_pick, (((2,), (1,)), ((0,), (0,))), precision=HIGH,
            preferred_element_type=jnp.float32,
        )

    halo_pick_all = jnp.stack([halo_low, halo_high, halo_bottom, halo_top])
    halo_dirs = [0, 1, 4, 5]
    spread_halo = np.concatenate(
        [select_np.T[:, f * pad_face : (f + 1) * pad_face] for f in halo_dirs], axis=1
    )
    square_halo = np.tile(square_np[:, 0], len(halo_dirs))
    into_state_np = DT_SQUARED * (spread_halo / cube_np) * (PENALTY * square_halo)[None, :]
    into_state = jnp.asarray(into_state_np, jnp.float32)
    into_faces = jnp.asarray(select_np @ into_state_np, jnp.float32)

    def halo_field(blocks):
        out = lax.dot_general(
            jnp.stack(blocks), halo_pick_all, (((2,), (1,)), ((0,), (0,))), precision=HIGH,
            preferred_element_type=jnp.float32,
        )
        return out.reshape(len(halo_dirs) * pad_face, elements)

    faces = mm(select, state).reshape(6, pad_face, 2 * elements)
    kernel_sum = jnp.zeros((pad_nodes, elements), jnp.float32)
    for step in range(STEPS):
        from_low = from_behind(faces[1], "group", 1)
        from_high = from_behind(faces[0], "group", -1)
        radial_face = jnp.where(depth_here == 0, faces[5], faces[4])
        from_radial = swapped(radial_face, "depth", 0)
        state, previous, faces, from_radial = lax.optimization_barrier(
            (state, previous, faces, from_radial)
        )
        grads = mm(grad_op, state).reshape(3, pad_nodes, 2 * elements)
        product = (
            grads[0][:, :elements] * grads[0][:, elements:]
            + grads[1][:, :elements] * grads[1][:, elements:]
            + grads[2][:, :elements] * grads[2][:, elements:]
        )
        kernel_sum = kernel_sum + KERNEL_SCALE * cube * speed_sq * product
        faces_sw = jnp.stack([faces[f ^ 1] for f in range(6)])
        other = jnp.concatenate(
            [own_part(faces_sw[..., :elements]), own_part(faces_sw[..., elements:])], axis=2
        )
        jumps = PENALTY * square * (faces - other)
        penal = mm(spread, jumps.reshape(6 * pad_face, 2 * elements))
        stiff = mm(stiff_op, (coef * grads).reshape(3 * pad_nodes, 2 * elements))
        partial = 2.0 * state - previous + DT_SQUARED * (-(stiff + penal) / cube)
        partial_faces = mm(select, partial)
        halo = jnp.concatenate(
            [
                halo_field([x[:, :elements] for x in (from_low, from_high, from_radial, from_radial)]),
                halo_field([x[:, elements:] for x in (from_low, from_high, from_radial, from_radial)]),
            ],
            axis=1,
        )
        faces = (partial_faces + mm(into_faces, halo)).reshape(6, pad_face, 2 * elements)
        previous = state
        state = partial + mm(into_state, halo)

    blocks = lax.dot_general(
        placer,
        kernel_sum[:NODES],
        (((1,), (1,)), ((), ())),
        precision=HIGH,
        preferred_element_type=jnp.float32,
    )
    packed = jnp.concatenate([blocks, labels[:, None]], axis=1)
    got = lax.all_to_all(packed, ("group", "depth"), 0, 0, tiled=True)
    got_labels = got[:, NODES] - 1.0
    cell_ids = jnp.arange(P_DEV, dtype=jnp.float32)[:, None]
    selector = (got_labels[None, :] == cell_ids).astype(jnp.float32)
    param_grad = mm(selector, got[:, :NODES])
    return (state[:NODES, :elements], state[:NODES, elements:], param_grad)


def solution(mesh):
    return jax.shard_map(
        per_device,
        mesh=mesh,
        in_specs=(
            P(None, ("group", "depth")),
            P(None, ("group", "depth")),
            P(None, ("group", "depth")),
            P(None, ("group", "depth")),
            P(("group", "depth")),
            P(None, ("group", "depth")),
            P(("group", "depth")),
            P(("group", "depth")),
            P(("group", "depth")),
            P(("group", "depth"), None),
            P(("group", "depth")),
        ),
        out_specs=(
            P(None, ("group", "depth")),
            P(None, ("group", "depth")),
            P(("group", "depth"), None),
        ),
        check_vma=False,
    )
```

```python
import math

import jax
import jax.numpy as jnp
import numpy as np
from jax import lax
from jax.sharding import PartitionSpec as P

NODES = 125
STEPS = 4
P_DEV = 128


PENALTY = 40.0
DT_SQUARED = 0.001
KERNEL_SCALE = 0.05
HIGH = lax.Precision.HIGHEST


def from_behind(block, axis, distance):
    devices = range(lax.axis_size(axis))
    route = [((i - distance) % len(devices), i) for i in devices]
    return lax.ppermute(block, axis, route)


def swapped(block, axis, apart):
    count = lax.axis_size(axis)
    route = []
    for low in range(count):
        high = low | 1 << apart
        if high != low and high < count:
            route += [(low, high), (high, low)]
    return lax.ppermute(block, axis, route)


def gll_tables():
    points = np.array([-1.0, -math.sqrt(3.0 / 7.0), 0.0, math.sqrt(3.0 / 7.0), 1.0])
    weights = np.array([0.1, 49.0 / 90.0, 32.0 / 45.0, 49.0 / 90.0, 0.1])
    barycentric = np.array(
        [np.prod([points[i] - points[m] for m in range(5) if m != i]) for i in range(5)]
    )
    derivative = np.zeros((5, 5))
    for i in range(5):
        for j in range(5):
            if i != j:
                derivative[i, j] = barycentric[i] / (barycentric[j] * (points[i] - points[j]))
            else:
                derivative[i, j] = sum((1.0 / (points[i] - points[m]) for m in range(5) if m != i))
    return (weights, derivative)


def node_tables():
    weights, derivative = gll_tables()
    single = np.eye(5)
    operators = [
        np.kron(derivative, np.kron(single, single)),
        np.kron(single, np.kron(derivative, single)),
        np.kron(single, np.kron(single, derivative)),
    ]
    cube = np.kron(weights, np.kron(weights, weights))
    digits = [(n // 25, n // 5 % 5, n % 5) for n in range(125)]
    rows = []
    for f in range(6):
        axis_pick = f // 2
        level = 0 if f % 2 == 0 else 4
        rows.append([n for n in range(125) if digits[n][axis_pick] == level])
    square = np.kron(weights, weights)
    spread = np.zeros((125, 150))
    for f in range(6):
        for a, n in enumerate(rows[f]):
            spread[n, 25 * f + a] = 1.0
    return (operators, cube, rows, square, spread)


def mm(a, b):
    return jnp.dot(a, b, precision=HIGH, preferred_element_type=jnp.float32)


def onehot(rows, index):
    return (jnp.arange(rows, dtype=jnp.int32)[:, None] == index[None, :]).astype(jnp.float32)


def padded_tables(pad_nodes, pad_face):
    operators, cube_np, rows, square_np, spread_np = node_tables()
    grad_op = np.zeros((3 * pad_nodes, pad_nodes))
    stiff_op = np.zeros((pad_nodes, 3 * pad_nodes))
    for d in range(3):
        grad_op[d * pad_nodes : d * pad_nodes + NODES, :NODES] = operators[d]
        stiff_op[:NODES, d * pad_nodes : d * pad_nodes + NODES] = operators[d].T
    select = np.zeros((6 * pad_face, pad_nodes))
    select_swapped = np.zeros((6 * pad_face, pad_nodes))
    for f in range(6):
        for a in range(25):
            select[f * pad_face + a, rows[f][a]] = 1.0
            select_swapped[f * pad_face + a, rows[f ^ 1][a]] = 1.0
    cube = np.ones((pad_nodes, 1))
    cube[:NODES, 0] = cube_np
    square = np.zeros((pad_face, 1))
    square[:25, 0] = square_np
    return grad_op, stiff_op, select, select_swapped, cube, square


def per_device(
    fwd_now,
    fwd_prev,
    adj_now,
    adj_prev,
    speed_sq,
    face_lists,
    send_low,
    send_high,
    send_radial,
    owner_dev,
    param_slot,
):
    pad_nodes, pad_face = 128, 32
    grad_np, stiff_np, select_np, select_sw_np, cube_np, square_np = padded_tables(
        pad_nodes, pad_face
    )
    elements = fwd_now.shape[1]
    groups = lax.axis_size("group")
    layers = lax.axis_size("depth")
    devices = groups * layers
    capacity = elements // devices + elements // (2 * devices) + 2
    radial_count = send_radial.shape[0]
    extra = pad_nodes - NODES

    def padded(a, b):
        return jnp.pad(jnp.concatenate([a, b], axis=1), ((0, extra), (0, 0)))

    state = padded(fwd_now, adj_now)
    previous = padded(fwd_prev, adj_prev)
    depth_here = lax.axis_index("depth")
    grad_op = jnp.asarray(grad_np, jnp.float32)
    stiff_op = jnp.asarray(stiff_np, jnp.float32)
    select = jnp.asarray(select_np, jnp.float32)
    select_swapped = jnp.asarray(select_sw_np, jnp.float32)
    spread = jnp.asarray(select_np.T, jnp.float32)
    cube = jnp.asarray(cube_np, jnp.float32)
    square = jnp.asarray(square_np, jnp.float32)
    speed2 = jnp.concatenate([speed_sq, speed_sq])
    coef = cube * speed2

    own_pick = jnp.stack([onehot(elements, face_lists[f]) for f in range(6)])

    def halo_pick(order, slots, lists):
        return mm(onehot(elements, order), onehot(slots, lists - elements))

    target = owner_dev[:, 0]
    counts = (target[:, None] == jnp.arange(devices, dtype=jnp.int32)[None, :]).astype(jnp.int32)
    before = jnp.cumsum(counts, axis=0) - counts
    position = jnp.sum(before * counts, axis=1)
    placing = target * capacity + position
    placer = onehot(devices * capacity, placing)
    labels = mm(placer, param_slot.astype(jnp.float32) + 1.0)

    def by_field(x, pick):
        return jnp.concatenate([mm(x[:, :elements], pick), mm(x[:, elements:], pick)], axis=1)

    def own_part(x):
        return lax.dot_general(
            x, own_pick, (((2,), (1,)), ((0,), (0,))), precision=HIGH,
            preferred_element_type=jnp.float32,
        )

    halo_dirs = [0, 1, 4, 5]
    spread_halo = np.concatenate(
        [select_np.T[:, f * pad_face : (f + 1) * pad_face] for f in halo_dirs], axis=1
    )
    square_halo = np.tile(square_np[:, 0], len(halo_dirs))
    into_state_np = DT_SQUARED * (spread_halo / cube_np) * (PENALTY * square_halo)[None, :]
    into_state = jnp.asarray(into_state_np, jnp.float32)
    into_faces = jnp.asarray(select_np @ into_state_np, jnp.float32)
    index_row = 25

    def with_index(face, order):
        return face.at[index_row, : order.shape[0]].set(order.astype(jnp.float32))

    def halo_field(blocks, picks):
        out = lax.dot_general(
            jnp.stack(blocks), picks, (((2,), (1,)), ((0,), (0,))), precision=HIGH,
            preferred_element_type=jnp.float32,
        )
        return out.reshape(len(halo_dirs) * pad_face, elements)

    faces = mm(select, state).reshape(6, pad_face, 2 * elements)
    kernel_sum = jnp.zeros((pad_nodes, elements), jnp.float32)
    pending = None
    halo_pick_all = None
    for step in range(STEPS):
        high_face, low_face = faces[1], faces[0]
        radial_face = jnp.where(depth_here == 0, faces[5], faces[4])
        if step == 0:
            high_face = with_index(high_face, send_high)
            low_face = with_index(low_face, send_low)
            radial_face = with_index(radial_face, send_radial)
        from_low = from_behind(high_face, "group", 1)
        from_high = from_behind(low_face, "group", -1)
        from_radial = swapped(radial_face, "depth", 0)
        if pending is None:
            state, previous, faces, from_radial = lax.optimization_barrier(
                (state, previous, faces, from_radial)
            )
        else:
            partial, halo, previous, faces, from_radial = lax.optimization_barrier(
                (*pending, previous, faces, from_radial)
            )
            state = partial + mm(into_state, halo)
        if halo_pick_all is None:
            def order_of(x, count):
                return x[index_row, :count].astype(jnp.int32)

            halo_pick_all = jnp.stack(
                [
                    halo_pick(order_of(from_low, elements), elements, face_lists[0]),
                    halo_pick(order_of(from_high, elements), elements, face_lists[1]),
                    halo_pick(order_of(from_radial, radial_count), radial_count, face_lists[4]),
                    halo_pick(order_of(from_radial, radial_count), radial_count, face_lists[5]),
                ]
            )
        grads = mm(grad_op, state).reshape(3, pad_nodes, 2 * elements)
        product = (
            grads[0][:, :elements] * grads[0][:, elements:]
            + grads[1][:, :elements] * grads[1][:, elements:]
            + grads[2][:, :elements] * grads[2][:, elements:]
        )
        kernel_sum = kernel_sum + KERNEL_SCALE * cube * speed_sq * product
        faces_sw = jnp.stack([faces[f ^ 1] for f in range(6)])
        other = jnp.concatenate(
            [own_part(faces_sw[..., :elements]), own_part(faces_sw[..., elements:])], axis=2
        )
        jumps = PENALTY * square * (faces - other)
        penal = mm(spread, jumps.reshape(6 * pad_face, 2 * elements))
        stiff = mm(stiff_op, (coef * grads).reshape(3 * pad_nodes, 2 * elements))
        partial = 2.0 * state - previous + DT_SQUARED * (-(stiff + penal) / cube)
        partial_faces = mm(select, partial)
        halos = (from_low, from_high, from_radial, from_radial)
        halo = jnp.concatenate(
            [
                halo_field([x[:, :elements] for x in halos], halo_pick_all),
                halo_field([x[:, elements:] for x in halos], halo_pick_all),
            ],
            axis=1,
        )
        faces = (partial_faces + mm(into_faces, halo)).reshape(6, pad_face, 2 * elements)
        previous = state
        pending = (partial, halo)
    state = pending[0] + mm(into_state, pending[1])

    blocks = lax.dot_general(
        placer,
        kernel_sum[:NODES],
        (((1,), (1,)), ((), ())),
        precision=HIGH,
        preferred_element_type=jnp.float32,
    )
    packed = jnp.concatenate([blocks, labels[:, None]], axis=1)
    got = lax.all_to_all(packed, ("group", "depth"), 0, 0, tiled=True)
    got_labels = got[:, NODES] - 1.0
    cell_ids = jnp.arange(P_DEV, dtype=jnp.float32)[:, None]
    selector = (got_labels[None, :] == cell_ids).astype(jnp.float32)
    param_grad = mm(selector, got[:, :NODES])
    return (state[:NODES, :elements], state[:NODES, elements:], param_grad)


def solution(mesh):
    return jax.shard_map(
        per_device,
        mesh=mesh,
        in_specs=(
            P(None, ("group", "depth")),
            P(None, ("group", "depth")),
            P(None, ("group", "depth")),
            P(None, ("group", "depth")),
            P(("group", "depth")),
            P(None, ("group", "depth")),
            P(("group", "depth")),
            P(("group", "depth")),
            P(("group", "depth")),
            P(("group", "depth"), None),
            P(("group", "depth")),
        ),
        out_specs=(
            P(None, ("group", "depth")),
            P(None, ("group", "depth")),
            P(("group", "depth"), None),
        ),
        check_vma=False,
    )
```

```python
import math

import jax
import jax.numpy as jnp
import numpy as np
from jax import lax
from jax.sharding import PartitionSpec as P

NODES = 125
STEPS = 4
P_DEV = 128


PENALTY = 40.0
DT_SQUARED = 0.001
KERNEL_SCALE = 0.05
HIGH = lax.Precision.HIGHEST


def from_behind(block, axis, distance):
    devices = range(lax.axis_size(axis))
    route = [((i - distance) % len(devices), i) for i in devices]
    return lax.ppermute(block, axis, route)


def swapped(block, axis, apart):
    count = lax.axis_size(axis)
    route = []
    for low in range(count):
        high = low | 1 << apart
        if high != low and high < count:
            route += [(low, high), (high, low)]
    return lax.ppermute(block, axis, route)


def gll_tables():
    points = np.array([-1.0, -math.sqrt(3.0 / 7.0), 0.0, math.sqrt(3.0 / 7.0), 1.0])
    weights = np.array([0.1, 49.0 / 90.0, 32.0 / 45.0, 49.0 / 90.0, 0.1])
    barycentric = np.array(
        [np.prod([points[i] - points[m] for m in range(5) if m != i]) for i in range(5)]
    )
    derivative = np.zeros((5, 5))
    for i in range(5):
        for j in range(5):
            if i != j:
                derivative[i, j] = barycentric[i] / (barycentric[j] * (points[i] - points[j]))
            else:
                derivative[i, j] = sum((1.0 / (points[i] - points[m]) for m in range(5) if m != i))
    return (weights, derivative)


def node_tables():
    weights, derivative = gll_tables()
    single = np.eye(5)
    operators = [
        np.kron(derivative, np.kron(single, single)),
        np.kron(single, np.kron(derivative, single)),
        np.kron(single, np.kron(single, derivative)),
    ]
    cube = np.kron(weights, np.kron(weights, weights))
    digits = [(n // 25, n // 5 % 5, n % 5) for n in range(125)]
    rows = []
    for f in range(6):
        axis_pick = f // 2
        level = 0 if f % 2 == 0 else 4
        rows.append([n for n in range(125) if digits[n][axis_pick] == level])
    square = np.kron(weights, weights)
    spread = np.zeros((125, 150))
    for f in range(6):
        for a, n in enumerate(rows[f]):
            spread[n, 25 * f + a] = 1.0
    return (operators, cube, rows, square, spread)


def mm(a, b):
    return jnp.dot(a, b, precision=HIGH, preferred_element_type=jnp.float32)


def onehot(rows, index):
    return (jnp.arange(rows, dtype=jnp.int32)[:, None] == index[None, :]).astype(jnp.float32)


def padded_tables(pad_nodes, pad_face):
    operators, cube_np, rows, square_np, spread_np = node_tables()
    grad_op = np.zeros((3 * pad_nodes, pad_nodes))
    stiff_op = np.zeros((pad_nodes, 3 * pad_nodes))
    for d in range(3):
        grad_op[d * pad_nodes : d * pad_nodes + NODES, :NODES] = operators[d]
        stiff_op[:NODES, d * pad_nodes : d * pad_nodes + NODES] = operators[d].T
    select = np.zeros((6 * pad_face, pad_nodes))
    select_swapped = np.zeros((6 * pad_face, pad_nodes))
    for f in range(6):
        for a in range(25):
            select[f * pad_face + a, rows[f][a]] = 1.0
            select_swapped[f * pad_face + a, rows[f ^ 1][a]] = 1.0
    cube = np.ones((pad_nodes, 1))
    cube[:NODES, 0] = cube_np
    square = np.zeros((pad_face, 1))
    square[:25, 0] = square_np
    return grad_op, stiff_op, select, select_swapped, cube, square


def per_device(
    fwd_now,
    fwd_prev,
    adj_now,
    adj_prev,
    speed_sq,
    face_lists,
    send_low,
    send_high,
    send_radial,
    owner_dev,
    param_slot,
):
    pad_nodes, pad_face = 128, 32
    grad_np, stiff_np, select_np, select_sw_np, cube_np, square_np = padded_tables(
        pad_nodes, pad_face
    )
    elements = fwd_now.shape[1]
    groups = lax.axis_size("group")
    layers = lax.axis_size("depth")
    devices = groups * layers
    capacity = elements // devices + elements // (2 * devices) + 2
    radial_count = send_radial.shape[0]
    extra = pad_nodes - NODES

    def padded(a, b):
        return jnp.pad(jnp.concatenate([a, b], axis=1), ((0, extra), (0, 0)))

    state = padded(fwd_now, adj_now)
    previous = padded(fwd_prev, adj_prev)
    depth_here = lax.axis_index("depth")
    grad_op = jnp.asarray(grad_np, jnp.float32)
    stiff_op = jnp.asarray(stiff_np, jnp.float32)
    select = jnp.asarray(select_np, jnp.float32)
    select_swapped = jnp.asarray(select_sw_np, jnp.float32)
    spread = jnp.asarray(select_np.T, jnp.float32)
    cube = jnp.asarray(cube_np, jnp.float32)
    square = jnp.asarray(square_np, jnp.float32)
    speed2 = jnp.concatenate([speed_sq, speed_sq])
    coef = cube * speed2

    own_pick = jnp.stack([onehot(elements, face_lists[f]) for f in range(6)])

    def halo_pick(order, slots, lists):
        return mm(onehot(elements, order), onehot(slots, lists - elements))

    target = owner_dev[:, 0]
    counts = (target[:, None] == jnp.arange(devices, dtype=jnp.int32)[None, :]).astype(jnp.int32)
    before = jnp.cumsum(counts, axis=0) - counts
    position = jnp.sum(before * counts, axis=1)
    placing = target * capacity + position
    placer = onehot(devices * capacity, placing)
    labels = mm(placer, param_slot.astype(jnp.float32) + 1.0)

    def by_field(x, pick):
        return jnp.concatenate([mm(x[:, :elements], pick), mm(x[:, elements:], pick)], axis=1)

    def own_part(x):
        return lax.dot_general(
            x, own_pick, (((2,), (1,)), ((0,), (0,))), precision=HIGH,
            preferred_element_type=jnp.float32,
        )

    halo_dirs = [0, 1, 4, 5]
    spread_halo = np.concatenate(
        [select_np.T[:, f * pad_face : (f + 1) * pad_face] for f in halo_dirs], axis=1
    )
    square_halo = np.tile(square_np[:, 0], len(halo_dirs))
    into_state_np = DT_SQUARED * (spread_halo / cube_np) * (PENALTY * square_halo)[None, :]
    into_state = jnp.asarray(into_state_np, jnp.float32)
    into_faces = jnp.asarray(select_np @ into_state_np, jnp.float32)
    index_row = 25

    def with_index(face, order):
        return face.at[index_row, : order.shape[0]].set(order.astype(jnp.float32))

    def halo_field(blocks, picks):
        out = lax.dot_general(
            jnp.stack(blocks), picks, (((2,), (1,)), ((0,), (0,))), precision=HIGH,
            preferred_element_type=jnp.float32,
        )
        return out.reshape(len(halo_dirs) * pad_face, elements)

    def exchange(faces, first, orders):
        high_face, low_face = faces[1], faces[0]
        radial_face = jnp.where(depth_here == 0, faces[5], faces[4])
        if first:
            high_face = with_index(high_face, orders[0])
            low_face = with_index(low_face, orders[1])
            radial_face = with_index(radial_face, orders[2])
        from_low = from_behind(high_face, "group", 1)
        from_high = from_behind(low_face, "group", -1)
        from_radial = swapped(radial_face, "depth", 0)
        return from_low, from_high, from_radial

    def local_work(state, previous, faces, kernel_sum, halos, picks):
        grads = mm(grad_op, state).reshape(3, pad_nodes, 2 * elements)
        product = (
            grads[0][:, :elements] * grads[0][:, elements:]
            + grads[1][:, :elements] * grads[1][:, elements:]
            + grads[2][:, :elements] * grads[2][:, elements:]
        )
        kernel_sum = kernel_sum + KERNEL_SCALE * cube * speed_sq * product
        faces_sw = jnp.stack([faces[f ^ 1] for f in range(6)])
        other = jnp.concatenate(
            [own_part(faces_sw[..., :elements]), own_part(faces_sw[..., elements:])], axis=2
        )
        jumps = PENALTY * square * (faces - other)
        penal = mm(spread, jumps.reshape(6 * pad_face, 2 * elements))
        stiff = mm(stiff_op, (coef * grads).reshape(3 * pad_nodes, 2 * elements))
        partial = 2.0 * state - previous + DT_SQUARED * (-(stiff + penal) / cube)
        partial_faces = mm(select, partial)
        halo = jnp.concatenate(
            [
                halo_field([x[:, :elements] for x in halos], picks),
                halo_field([x[:, elements:] for x in halos], picks),
            ],
            axis=1,
        )
        faces = (partial_faces + mm(into_faces, halo)).reshape(6, pad_face, 2 * elements)
        return partial, halo, faces, kernel_sum

    def order_of(x, count):
        return x[index_row, :count].astype(jnp.int32)

    faces = mm(select, state).reshape(6, pad_face, 2 * elements)
    kernel_sum = jnp.zeros((pad_nodes, elements), jnp.float32)
    from_low, from_high, from_radial = exchange(faces, True, (send_high, send_low, send_radial))
    state, previous, faces, from_radial = lax.optimization_barrier(
        (state, previous, faces, from_radial)
    )
    halo_pick_all = jnp.stack(
        [
            halo_pick(order_of(from_low, elements), elements, face_lists[0]),
            halo_pick(order_of(from_high, elements), elements, face_lists[1]),
            halo_pick(order_of(from_radial, radial_count), radial_count, face_lists[4]),
            halo_pick(order_of(from_radial, radial_count), radial_count, face_lists[5]),
        ]
    )
    halos = (from_low, from_high, from_radial, from_radial)
    partial, halo, faces, kernel_sum = local_work(
        state, previous, faces, kernel_sum, halos, halo_pick_all
    )
    previous = state

    def later_step(step, carry):
        partial, halo, previous, faces, kernel_sum = carry
        from_low, from_high, from_radial = exchange(faces, False, None)
        partial, halo, previous, faces, from_radial = lax.optimization_barrier(
            (partial, halo, previous, faces, from_radial)
        )
        state = partial + mm(into_state, halo)
        halos = (from_low, from_high, from_radial, from_radial)
        partial, halo, faces, kernel_sum = local_work(
            state, previous, faces, kernel_sum, halos, halo_pick_all
        )
        return (partial, halo, state, faces, kernel_sum)

    partial, halo, previous, faces, kernel_sum = lax.fori_loop(
        1, STEPS, later_step, (partial, halo, previous, faces, kernel_sum)
    )
    state = partial + mm(into_state, halo)

    blocks = lax.dot_general(
        placer,
        kernel_sum[:NODES],
        (((1,), (1,)), ((), ())),
        precision=HIGH,
        preferred_element_type=jnp.float32,
    )
    packed = jnp.concatenate([blocks, labels[:, None]], axis=1)
    got = lax.all_to_all(packed, ("group", "depth"), 0, 0, tiled=True)
    got_labels = got[:, NODES] - 1.0
    cell_ids = jnp.arange(P_DEV, dtype=jnp.float32)[:, None]
    selector = (got_labels[None, :] == cell_ids).astype(jnp.float32)
    param_grad = mm(selector, got[:, :NODES])
    return (state[:NODES, :elements], state[:NODES, elements:], param_grad)


def solution(mesh):
    return jax.shard_map(
        per_device,
        mesh=mesh,
        in_specs=(
            P(None, ("group", "depth")),
            P(None, ("group", "depth")),
            P(None, ("group", "depth")),
            P(None, ("group", "depth")),
            P(("group", "depth")),
            P(None, ("group", "depth")),
            P(("group", "depth")),
            P(("group", "depth")),
            P(("group", "depth")),
            P(("group", "depth"), None),
            P(("group", "depth")),
        ),
        out_specs=(
            P(None, ("group", "depth")),
            P(None, ("group", "depth")),
            P(("group", "depth"), None),
        ),
        check_vma=False,
    )
```

```python
import math

import jax
import jax.numpy as jnp
import numpy as np
from jax import lax
from jax.sharding import PartitionSpec as P

NODES = 125
STEPS = 4
P_DEV = 128


PENALTY = 40.0
DT_SQUARED = 0.001
KERNEL_SCALE = 0.05
HIGH = lax.Precision.HIGHEST


def from_behind(block, axis, distance):
    devices = range(lax.axis_size(axis))
    route = [((i - distance) % len(devices), i) for i in devices]
    return lax.ppermute(block, axis, route)


def swapped(block, axis, apart):
    count = lax.axis_size(axis)
    route = []
    for low in range(count):
        high = low | 1 << apart
        if high != low and high < count:
            route += [(low, high), (high, low)]
    return lax.ppermute(block, axis, route)


def gll_tables():
    points = np.array([-1.0, -math.sqrt(3.0 / 7.0), 0.0, math.sqrt(3.0 / 7.0), 1.0])
    weights = np.array([0.1, 49.0 / 90.0, 32.0 / 45.0, 49.0 / 90.0, 0.1])
    barycentric = np.array(
        [np.prod([points[i] - points[m] for m in range(5) if m != i]) for i in range(5)]
    )
    derivative = np.zeros((5, 5))
    for i in range(5):
        for j in range(5):
            if i != j:
                derivative[i, j] = barycentric[i] / (barycentric[j] * (points[i] - points[j]))
            else:
                derivative[i, j] = sum((1.0 / (points[i] - points[m]) for m in range(5) if m != i))
    return (weights, derivative)


def node_tables():
    weights, derivative = gll_tables()
    single = np.eye(5)
    operators = [
        np.kron(derivative, np.kron(single, single)),
        np.kron(single, np.kron(derivative, single)),
        np.kron(single, np.kron(single, derivative)),
    ]
    cube = np.kron(weights, np.kron(weights, weights))
    digits = [(n // 25, n // 5 % 5, n % 5) for n in range(125)]
    rows = []
    for f in range(6):
        axis_pick = f // 2
        level = 0 if f % 2 == 0 else 4
        rows.append([n for n in range(125) if digits[n][axis_pick] == level])
    square = np.kron(weights, weights)
    spread = np.zeros((125, 150))
    for f in range(6):
        for a, n in enumerate(rows[f]):
            spread[n, 25 * f + a] = 1.0
    return (operators, cube, rows, square, spread)


def mm(a, b):
    return jnp.dot(a, b, precision=HIGH, preferred_element_type=jnp.float32)


def onehot(rows, index):
    return (jnp.arange(rows, dtype=jnp.int32)[:, None] == index[None, :]).astype(jnp.float32)


def padded_tables(pad_nodes, pad_face):
    operators, cube_np, rows, square_np, spread_np = node_tables()
    grad_op = np.zeros((3 * pad_nodes, pad_nodes))
    stiff_op = np.zeros((pad_nodes, 3 * pad_nodes))
    for d in range(3):
        grad_op[d * pad_nodes : d * pad_nodes + NODES, :NODES] = operators[d]
        stiff_op[:NODES, d * pad_nodes : d * pad_nodes + NODES] = operators[d].T
    select = np.zeros((6 * pad_face, pad_nodes))
    select_swapped = np.zeros((6 * pad_face, pad_nodes))
    for f in range(6):
        for a in range(25):
            select[f * pad_face + a, rows[f][a]] = 1.0
            select_swapped[f * pad_face + a, rows[f ^ 1][a]] = 1.0
    cube = np.ones((pad_nodes, 1))
    cube[:NODES, 0] = cube_np
    square = np.zeros((pad_face, 1))
    square[:25, 0] = square_np
    return grad_op, stiff_op, select, select_swapped, cube, square


def per_device(
    fwd_now,
    fwd_prev,
    adj_now,
    adj_prev,
    speed_sq,
    face_lists,
    send_low,
    send_high,
    send_radial,
    owner_dev,
    param_slot,
):
    pad_nodes, pad_face = 128, 32
    grad_np, stiff_np, select_np, select_sw_np, cube_np, square_np = padded_tables(
        pad_nodes, pad_face
    )
    elements = fwd_now.shape[1]
    groups = lax.axis_size("group")
    layers = lax.axis_size("depth")
    devices = groups * layers
    capacity = elements // devices + elements // (2 * devices) + 2
    radial_count = send_radial.shape[0]
    extra = pad_nodes - NODES

    def padded(a, b):
        return jnp.pad(jnp.concatenate([a, b], axis=1), ((0, extra), (0, 0)))

    state = padded(fwd_now, adj_now)
    previous = padded(fwd_prev, adj_prev)
    depth_here = lax.axis_index("depth")
    grad_op = jnp.asarray(grad_np, jnp.float32)
    stiff_op = jnp.asarray(stiff_np, jnp.float32)
    select = jnp.asarray(select_np, jnp.float32)
    select_swapped = jnp.asarray(select_sw_np, jnp.float32)
    spread = jnp.asarray(select_np.T, jnp.float32)
    cube = jnp.asarray(cube_np, jnp.float32)
    square = jnp.asarray(square_np, jnp.float32)
    speed2 = jnp.concatenate([speed_sq, speed_sq])
    coef = cube * speed2

    own_pick = jnp.stack([onehot(elements, face_lists[f]) for f in range(6)]).astype(jnp.bfloat16)

    def halo_pick(order, slots, lists):
        return mm(onehot(elements, order), onehot(slots, lists - elements))

    target = owner_dev[:, 0]
    counts = (target[:, None] == jnp.arange(devices, dtype=jnp.int32)[None, :]).astype(jnp.int32)
    before = jnp.cumsum(counts, axis=0) - counts
    position = jnp.sum(before * counts, axis=1)
    placing = target * capacity + position
    placer = onehot(devices * capacity, placing)
    labels = mm(placer, param_slot.astype(jnp.float32) + 1.0)

    def by_field(x, pick):
        return jnp.concatenate([mm(x[:, :elements], pick), mm(x[:, elements:], pick)], axis=1)

    def own_part(x):
        return lax.dot_general(
            x, own_pick, (((2,), (1,)), ((0,), (0,))), precision=HIGH,
            preferred_element_type=jnp.float32,
        )

    halo_dirs = [0, 1, 4, 5]
    spread_halo = np.concatenate(
        [select_np.T[:, f * pad_face : (f + 1) * pad_face] for f in halo_dirs], axis=1
    )
    square_halo = np.tile(square_np[:, 0], len(halo_dirs))
    into_state_np = DT_SQUARED * (spread_halo / cube_np) * (PENALTY * square_halo)[None, :]
    into_state = jnp.asarray(into_state_np, jnp.float32)
    into_faces = jnp.asarray(select_np @ into_state_np, jnp.float32)
    index_row = 25

    def with_index(face, order):
        return face.at[index_row, : order.shape[0]].set(order.astype(jnp.float32))

    def split_pick(x, picks):
        rows = x.shape[1]
        fields = jnp.concatenate([x[..., :elements], x[..., elements:]], axis=1)
        hi = lax.reduce_precision(fields, exponent_bits=8, mantissa_bits=7)
        rest = fields - hi
        mid = lax.reduce_precision(rest, exponent_bits=8, mantissa_bits=7)
        lo = rest - mid
        parts = jnp.concatenate([hi, mid, lo], axis=1).astype(jnp.bfloat16)
        out = lax.dot_general(
            parts, picks, (((2,), (1,)), ((0,), (0,))),
            preferred_element_type=jnp.float32,
        )
        whole = out[:, : 2 * rows] + out[:, 2 * rows : 4 * rows] + out[:, 4 * rows :]
        return whole[:, :rows], whole[:, rows:]

    def halo_field(blocks, picks):
        u, v = split_pick(jnp.stack(blocks), picks)
        count = len(blocks) * pad_face
        return jnp.concatenate([u.reshape(count, elements), v.reshape(count, elements)], axis=1)

    faces = mm(select, state).reshape(6, pad_face, 2 * elements)
    kernel_sum = jnp.zeros((pad_nodes, elements), jnp.float32)
    pending = None
    halo_pick_all = None
    for step in range(STEPS):
        high_face, low_face = faces[1], faces[0]
        radial_face = jnp.where(depth_here == 0, faces[5], faces[4])
        if step == 0:
            high_face = with_index(high_face, send_high)
            low_face = with_index(low_face, send_low)
            radial_face = with_index(radial_face, send_radial)
        from_low = from_behind(high_face, "group", 1)
        from_high = from_behind(low_face, "group", -1)
        from_radial = swapped(radial_face, "depth", 0)
        if pending is None:
            state, previous, faces, from_radial = lax.optimization_barrier(
                (state, previous, faces, from_radial)
            )
        else:
            partial, halo, previous, faces, from_radial = lax.optimization_barrier(
                (*pending, previous, faces, from_radial)
            )
            state = partial + mm(into_state, halo)
        if halo_pick_all is None:
            def order_of(x, count):
                return x[index_row, :count].astype(jnp.int32)

            halo_pick_all = jnp.stack(
                [
                    halo_pick(order_of(from_low, elements), elements, face_lists[0]),
                    halo_pick(order_of(from_high, elements), elements, face_lists[1]),
                    halo_pick(order_of(from_radial, radial_count), radial_count, face_lists[4]),
                    halo_pick(order_of(from_radial, radial_count), radial_count, face_lists[5]),
                ]
            ).astype(jnp.bfloat16)
        grads = mm(grad_op, state).reshape(3, pad_nodes, 2 * elements)
        product = (
            grads[0][:, :elements] * grads[0][:, elements:]
            + grads[1][:, :elements] * grads[1][:, elements:]
            + grads[2][:, :elements] * grads[2][:, elements:]
        )
        kernel_sum = kernel_sum + KERNEL_SCALE * cube * speed_sq * product
        faces_sw = jnp.stack([faces[f ^ 1] for f in range(6)])
        other = jnp.concatenate(split_pick(faces_sw, own_pick), axis=2)
        jumps = PENALTY * square * (faces - other)
        penal = mm(spread, jumps.reshape(6 * pad_face, 2 * elements))
        stiff = mm(stiff_op, (coef * grads).reshape(3 * pad_nodes, 2 * elements))
        partial = 2.0 * state - previous + DT_SQUARED * (-(stiff + penal) / cube)
        partial_faces = mm(select, partial)
        halos = (from_low, from_high, from_radial, from_radial)
        halo = halo_field(list(halos), halo_pick_all)
        faces = (partial_faces + mm(into_faces, halo)).reshape(6, pad_face, 2 * elements)
        previous = state
        pending = (partial, halo)
    state = pending[0] + mm(into_state, pending[1])

    blocks = lax.dot_general(
        placer,
        kernel_sum[:NODES],
        (((1,), (1,)), ((), ())),
        precision=HIGH,
        preferred_element_type=jnp.float32,
    )
    packed = jnp.concatenate([blocks, labels[:, None]], axis=1)
    got = lax.all_to_all(packed, ("group", "depth"), 0, 0, tiled=True)
    got_labels = got[:, NODES] - 1.0
    cell_ids = jnp.arange(P_DEV, dtype=jnp.float32)[:, None]
    selector = (got_labels[None, :] == cell_ids).astype(jnp.float32)
    param_grad = mm(selector, got[:, :NODES])
    return (state[:NODES, :elements], state[:NODES, elements:], param_grad)


def solution(mesh):
    return jax.shard_map(
        per_device,
        mesh=mesh,
        in_specs=(
            P(None, ("group", "depth")),
            P(None, ("group", "depth")),
            P(None, ("group", "depth")),
            P(None, ("group", "depth")),
            P(("group", "depth")),
            P(None, ("group", "depth")),
            P(("group", "depth")),
            P(("group", "depth")),
            P(("group", "depth")),
            P(("group", "depth"), None),
            P(("group", "depth")),
        ),
        out_specs=(
            P(None, ("group", "depth")),
            P(None, ("group", "depth")),
            P(("group", "depth"), None),
        ),
        check_vma=False,
    )
```

```python
import math

import jax
import jax.numpy as jnp
import numpy as np
from jax import lax
from jax.sharding import PartitionSpec as P

NODES = 125
STEPS = 4
P_DEV = 128


PENALTY = 40.0
DT_SQUARED = 0.001
KERNEL_SCALE = 0.05
HIGH = lax.Precision.HIGHEST


def from_behind(block, axis, distance):
    devices = range(lax.axis_size(axis))
    route = [((i - distance) % len(devices), i) for i in devices]
    return lax.ppermute(block, axis, route)


def swapped(block, axis, apart):
    count = lax.axis_size(axis)
    route = []
    for low in range(count):
        high = low | 1 << apart
        if high != low and high < count:
            route += [(low, high), (high, low)]
    return lax.ppermute(block, axis, route)


def gll_tables():
    points = np.array([-1.0, -math.sqrt(3.0 / 7.0), 0.0, math.sqrt(3.0 / 7.0), 1.0])
    weights = np.array([0.1, 49.0 / 90.0, 32.0 / 45.0, 49.0 / 90.0, 0.1])
    barycentric = np.array(
        [np.prod([points[i] - points[m] for m in range(5) if m != i]) for i in range(5)]
    )
    derivative = np.zeros((5, 5))
    for i in range(5):
        for j in range(5):
            if i != j:
                derivative[i, j] = barycentric[i] / (barycentric[j] * (points[i] - points[j]))
            else:
                derivative[i, j] = sum((1.0 / (points[i] - points[m]) for m in range(5) if m != i))
    return (weights, derivative)


def node_tables():
    weights, derivative = gll_tables()
    single = np.eye(5)
    operators = [
        np.kron(derivative, np.kron(single, single)),
        np.kron(single, np.kron(derivative, single)),
        np.kron(single, np.kron(single, derivative)),
    ]
    cube = np.kron(weights, np.kron(weights, weights))
    digits = [(n // 25, n // 5 % 5, n % 5) for n in range(125)]
    rows = []
    for f in range(6):
        axis_pick = f // 2
        level = 0 if f % 2 == 0 else 4
        rows.append([n for n in range(125) if digits[n][axis_pick] == level])
    square = np.kron(weights, weights)
    spread = np.zeros((125, 150))
    for f in range(6):
        for a, n in enumerate(rows[f]):
            spread[n, 25 * f + a] = 1.0
    return (operators, cube, rows, square, spread)


def mm(a, b):
    return jnp.dot(a, b, precision=HIGH, preferred_element_type=jnp.float32)


def onehot(rows, index):
    return (jnp.arange(rows, dtype=jnp.int32)[:, None] == index[None, :]).astype(jnp.float32)


def padded_tables(pad_nodes, pad_face):
    operators, cube_np, rows, square_np, spread_np = node_tables()
    grad_op = np.zeros((3 * pad_nodes, pad_nodes))
    stiff_op = np.zeros((pad_nodes, 3 * pad_nodes))
    for d in range(3):
        grad_op[d * pad_nodes : d * pad_nodes + NODES, :NODES] = operators[d]
        stiff_op[:NODES, d * pad_nodes : d * pad_nodes + NODES] = operators[d].T
    select = np.zeros((6 * pad_face, pad_nodes))
    select_swapped = np.zeros((6 * pad_face, pad_nodes))
    for f in range(6):
        for a in range(25):
            select[f * pad_face + a, rows[f][a]] = 1.0
            select_swapped[f * pad_face + a, rows[f ^ 1][a]] = 1.0
    cube = np.ones((pad_nodes, 1))
    cube[:NODES, 0] = cube_np
    square = np.zeros((pad_face, 1))
    square[:25, 0] = square_np
    return grad_op, stiff_op, select, select_swapped, cube, square


def per_device(
    fwd_now,
    fwd_prev,
    adj_now,
    adj_prev,
    speed_sq,
    face_lists,
    send_low,
    send_high,
    send_radial,
    owner_dev,
    param_slot,
):
    pad_nodes, pad_face = 128, 32
    grad_np, stiff_np, select_np, select_sw_np, cube_np, square_np = padded_tables(
        pad_nodes, pad_face
    )
    elements = fwd_now.shape[1]
    groups = lax.axis_size("group")
    layers = lax.axis_size("depth")
    devices = groups * layers
    capacity = elements // devices + elements // (2 * devices) + 2
    radial_count = send_radial.shape[0]
    extra = pad_nodes - NODES

    def padded(a, b):
        return jnp.pad(jnp.concatenate([a, b], axis=1), ((0, extra), (0, 0)))

    state = padded(fwd_now, adj_now)
    previous = padded(fwd_prev, adj_prev)
    depth_here = lax.axis_index("depth")
    grad_op = jnp.asarray(grad_np, jnp.float32)
    stiff_op = jnp.asarray(stiff_np, jnp.float32)
    select = jnp.asarray(select_np, jnp.float32)
    select_swapped = jnp.asarray(select_sw_np, jnp.float32)
    spread = jnp.asarray(select_np.T, jnp.float32)
    cube = jnp.asarray(cube_np, jnp.float32)
    square = jnp.asarray(square_np, jnp.float32)
    speed2 = jnp.concatenate([speed_sq, speed_sq])
    coef = cube * speed2

    own_pick = jnp.stack([onehot(elements, face_lists[f]) for f in range(6)])

    def halo_pick(order, slots, lists):
        return mm(onehot(elements, order), onehot(slots, lists - elements))

    target = owner_dev[:, 0]
    counts = (target[:, None] == jnp.arange(devices, dtype=jnp.int32)[None, :]).astype(jnp.int32)
    before = jnp.cumsum(counts, axis=0) - counts
    position = jnp.sum(before * counts, axis=1)
    placing = target * capacity + position
    placer = onehot(devices * capacity, placing)
    labels = mm(placer, param_slot.astype(jnp.float32) + 1.0)

    def by_field(x, pick):
        return jnp.concatenate([mm(x[:, :elements], pick), mm(x[:, elements:], pick)], axis=1)

    def own_part(x):
        return lax.dot_general(
            x, own_pick, (((2,), (1,)), ((0,), (0,))), precision=HIGH,
            preferred_element_type=jnp.float32,
        )

    halo_dirs = [0, 1, 4, 5]
    spread_halo = np.concatenate(
        [select_np.T[:, f * pad_face : (f + 1) * pad_face] for f in halo_dirs], axis=1
    )
    square_halo = np.tile(square_np[:, 0], len(halo_dirs))
    into_state_np = DT_SQUARED * (spread_halo / cube_np) * (PENALTY * square_halo)[None, :]
    into_state = jnp.asarray(into_state_np, jnp.float32)
    into_faces = jnp.asarray(select_np @ into_state_np, jnp.float32)
    index_row = 25

    def with_index(face, order):
        return face.at[index_row, : order.shape[0]].set(order.astype(jnp.float32))

    def halo_field(blocks, picks):
        x = jnp.stack(blocks)
        rows = x.shape[1]
        fields = jnp.concatenate([x[..., :elements], x[..., elements:]], axis=1)
        hi = lax.reduce_precision(fields, exponent_bits=8, mantissa_bits=7)
        rest = fields - hi
        mid = lax.reduce_precision(rest, exponent_bits=8, mantissa_bits=7)
        lo = rest - mid
        parts = jnp.concatenate([hi, mid, lo], axis=1).astype(jnp.bfloat16)
        out = lax.dot_general(
            parts, picks, (((2,), (1,)), ((0,), (0,))), preferred_element_type=jnp.float32,
        )
        whole = out[:, : 2 * rows] + out[:, 2 * rows : 4 * rows] + out[:, 4 * rows :]
        count = len(blocks) * pad_face
        return jnp.concatenate(
            [whole[:, :rows].reshape(count, elements), whole[:, rows:].reshape(count, elements)],
            axis=1,
        )

    faces = mm(select, state).reshape(6, pad_face, 2 * elements)
    kernel_sum = jnp.zeros((pad_nodes, elements), jnp.float32)
    pending = None
    halo_pick_all = None
    for step in range(STEPS):
        high_face, low_face = faces[1], faces[0]
        radial_face = jnp.where(depth_here == 0, faces[5], faces[4])
        if step == 0:
            high_face = with_index(high_face, send_high)
            low_face = with_index(low_face, send_low)
            radial_face = with_index(radial_face, send_radial)
        from_low = from_behind(high_face, "group", 1)
        from_high = from_behind(low_face, "group", -1)
        from_radial = swapped(radial_face, "depth", 0)
        if pending is None:
            state, previous, faces, from_radial = lax.optimization_barrier(
                (state, previous, faces, from_radial)
            )
        else:
            partial, halo, previous, faces, from_radial = lax.optimization_barrier(
                (*pending, previous, faces, from_radial)
            )
            state = partial + mm(into_state, halo)
        if halo_pick_all is None:
            def order_of(x, count):
                return x[index_row, :count].astype(jnp.int32)

            halo_pick_all = jnp.stack(
                [
                    halo_pick(order_of(from_low, elements), elements, face_lists[0]),
                    halo_pick(order_of(from_high, elements), elements, face_lists[1]),
                    halo_pick(order_of(from_radial, radial_count), radial_count, face_lists[4]),
                    halo_pick(order_of(from_radial, radial_count), radial_count, face_lists[5]),
                ]
            ).astype(jnp.bfloat16)
        grads = mm(grad_op, state).reshape(3, pad_nodes, 2 * elements)
        product = (
            grads[0][:, :elements] * grads[0][:, elements:]
            + grads[1][:, :elements] * grads[1][:, elements:]
            + grads[2][:, :elements] * grads[2][:, elements:]
        )
        kernel_sum = kernel_sum + KERNEL_SCALE * cube * speed_sq * product
        faces_sw = jnp.stack([faces[f ^ 1] for f in range(6)])
        other = jnp.concatenate(
            [own_part(faces_sw[..., :elements]), own_part(faces_sw[..., elements:])], axis=2
        )
        jumps = PENALTY * square * (faces - other)
        penal = mm(spread, jumps.reshape(6 * pad_face, 2 * elements))
        stiff = mm(stiff_op, (coef * grads).reshape(3 * pad_nodes, 2 * elements))
        partial = 2.0 * state - previous + DT_SQUARED * (-(stiff + penal) / cube)
        partial_faces = mm(select, partial)
        halos = (from_low, from_high, from_radial, from_radial)
        halo = halo_field(list(halos), halo_pick_all)
        faces = (partial_faces + mm(into_faces, halo)).reshape(6, pad_face, 2 * elements)
        previous = state
        pending = (partial, halo)
    state = pending[0] + mm(into_state, pending[1])

    blocks = lax.dot_general(
        placer,
        kernel_sum[:NODES],
        (((1,), (1,)), ((), ())),
        precision=HIGH,
        preferred_element_type=jnp.float32,
    )
    packed = jnp.concatenate([blocks, labels[:, None]], axis=1)
    got = lax.all_to_all(packed, ("group", "depth"), 0, 0, tiled=True)
    got_labels = got[:, NODES] - 1.0
    cell_ids = jnp.arange(P_DEV, dtype=jnp.float32)[:, None]
    selector = (got_labels[None, :] == cell_ids).astype(jnp.float32)
    param_grad = mm(selector, got[:, :NODES])
    return (state[:NODES, :elements], state[:NODES, elements:], param_grad)


def solution(mesh):
    return jax.shard_map(
        per_device,
        mesh=mesh,
        in_specs=(
            P(None, ("group", "depth")),
            P(None, ("group", "depth")),
            P(None, ("group", "depth")),
            P(None, ("group", "depth")),
            P(("group", "depth")),
            P(None, ("group", "depth")),
            P(("group", "depth")),
            P(("group", "depth")),
            P(("group", "depth")),
            P(("group", "depth"), None),
            P(("group", "depth")),
        ),
        out_specs=(
            P(None, ("group", "depth")),
            P(None, ("group", "depth")),
            P(("group", "depth"), None),
        ),
        check_vma=False,
    )
```

```python
import math

import jax
import jax.numpy as jnp
import numpy as np
from jax import lax
from jax.sharding import PartitionSpec as P

NODES = 125
STEPS = 4
P_DEV = 128


PENALTY = 40.0
DT_SQUARED = 0.001
KERNEL_SCALE = 0.05
HIGH = lax.Precision.HIGHEST


def from_behind(block, axis, distance):
    devices = range(lax.axis_size(axis))
    route = [((i - distance) % len(devices), i) for i in devices]
    return lax.ppermute(block, axis, route)


def swapped(block, axis, apart):
    count = lax.axis_size(axis)
    route = []
    for low in range(count):
        high = low | 1 << apart
        if high != low and high < count:
            route += [(low, high), (high, low)]
    return lax.ppermute(block, axis, route)


def gll_tables():
    points = np.array([-1.0, -math.sqrt(3.0 / 7.0), 0.0, math.sqrt(3.0 / 7.0), 1.0])
    weights = np.array([0.1, 49.0 / 90.0, 32.0 / 45.0, 49.0 / 90.0, 0.1])
    barycentric = np.array(
        [np.prod([points[i] - points[m] for m in range(5) if m != i]) for i in range(5)]
    )
    derivative = np.zeros((5, 5))
    for i in range(5):
        for j in range(5):
            if i != j:
                derivative[i, j] = barycentric[i] / (barycentric[j] * (points[i] - points[j]))
            else:
                derivative[i, j] = sum((1.0 / (points[i] - points[m]) for m in range(5) if m != i))
    return (weights, derivative)


def node_tables():
    weights, derivative = gll_tables()
    single = np.eye(5)
    operators = [
        np.kron(derivative, np.kron(single, single)),
        np.kron(single, np.kron(derivative, single)),
        np.kron(single, np.kron(single, derivative)),
    ]
    cube = np.kron(weights, np.kron(weights, weights))
    digits = [(n // 25, n // 5 % 5, n % 5) for n in range(125)]
    rows = []
    for f in range(6):
        axis_pick = f // 2
        level = 0 if f % 2 == 0 else 4
        rows.append([n for n in range(125) if digits[n][axis_pick] == level])
    square = np.kron(weights, weights)
    spread = np.zeros((125, 150))
    for f in range(6):
        for a, n in enumerate(rows[f]):
            spread[n, 25 * f + a] = 1.0
    return (operators, cube, rows, square, spread)


def mm(a, b):
    return jnp.dot(a, b, precision=HIGH, preferred_element_type=jnp.float32)


def onehot(rows, index):
    return (jnp.arange(rows, dtype=jnp.int32)[:, None] == index[None, :]).astype(jnp.float32)


def padded_tables(pad_nodes, pad_face):
    operators, cube_np, rows, square_np, spread_np = node_tables()
    grad_op = np.zeros((3 * pad_nodes, pad_nodes))
    stiff_op = np.zeros((pad_nodes, 3 * pad_nodes))
    for d in range(3):
        grad_op[d * pad_nodes : d * pad_nodes + NODES, :NODES] = operators[d]
        stiff_op[:NODES, d * pad_nodes : d * pad_nodes + NODES] = operators[d].T
    select = np.zeros((6 * pad_face, pad_nodes))
    select_swapped = np.zeros((6 * pad_face, pad_nodes))
    for f in range(6):
        for a in range(25):
            select[f * pad_face + a, rows[f][a]] = 1.0
            select_swapped[f * pad_face + a, rows[f ^ 1][a]] = 1.0
    cube = np.ones((pad_nodes, 1))
    cube[:NODES, 0] = cube_np
    square = np.zeros((pad_face, 1))
    square[:25, 0] = square_np
    return grad_op, stiff_op, select, select_swapped, cube, square


def per_device(
    fwd_now,
    fwd_prev,
    adj_now,
    adj_prev,
    speed_sq,
    face_lists,
    send_low,
    send_high,
    send_radial,
    owner_dev,
    param_slot,
):
    pad_nodes, pad_face = 128, 32
    grad_np, stiff_np, select_np, select_sw_np, cube_np, square_np = padded_tables(
        pad_nodes, pad_face
    )
    elements = fwd_now.shape[1]
    groups = lax.axis_size("group")
    layers = lax.axis_size("depth")
    devices = groups * layers
    capacity = elements // devices + elements // (2 * devices) + 2
    radial_count = send_radial.shape[0]
    extra = pad_nodes - NODES

    def padded(a, b):
        return jnp.pad(jnp.concatenate([a, b], axis=1), ((0, extra), (0, 0)))

    state = padded(fwd_now, adj_now)
    previous = padded(fwd_prev, adj_prev)
    depth_here = lax.axis_index("depth")
    grad_op = jnp.asarray(grad_np, jnp.float32)
    stiff_op = jnp.asarray(stiff_np, jnp.float32)
    select = jnp.asarray(select_np, jnp.float32)
    select_swapped = jnp.asarray(select_sw_np, jnp.float32)
    spread = jnp.asarray(select_np.T, jnp.float32)
    cube = jnp.asarray(cube_np, jnp.float32)
    square = jnp.asarray(square_np, jnp.float32)
    speed2 = jnp.concatenate([speed_sq, speed_sq])
    coef = cube * speed2

    own_pick = jnp.stack([onehot(elements, face_lists[f]) for f in range(6)])

    def halo_pick(order, slots, lists):
        return mm(onehot(elements, order), onehot(slots, lists - elements))

    target = owner_dev[:, 0]
    counts = (target[:, None] == jnp.arange(devices, dtype=jnp.int32)[None, :]).astype(jnp.int32)
    before = jnp.cumsum(counts, axis=0) - counts
    position = jnp.sum(before * counts, axis=1)
    placing = target * capacity + position
    placer = onehot(devices * capacity, placing)
    labels = mm(placer, param_slot.astype(jnp.float32) + 1.0)

    def by_field(x, pick):
        return jnp.concatenate([mm(x[:, :elements], pick), mm(x[:, elements:], pick)], axis=1)

    def own_part(x):
        return lax.dot_general(
            x, own_pick, (((2,), (1,)), ((0,), (0,))), precision=HIGH,
            preferred_element_type=jnp.float32,
        )

    halo_dirs = [0, 1, 4, 5]
    spread_halo = np.concatenate(
        [select_np.T[:, f * pad_face : (f + 1) * pad_face] for f in halo_dirs], axis=1
    )
    square_halo = np.tile(square_np[:, 0], len(halo_dirs))
    into_state_np = DT_SQUARED * (spread_halo / cube_np) * (PENALTY * square_halo)[None, :]
    into_state = jnp.asarray(into_state_np, jnp.float32)
    into_faces = jnp.asarray(select_np @ into_state_np, jnp.float32)
    index_row = 25

    def with_index(face, order):
        return face.at[index_row, : order.shape[0]].set(order.astype(jnp.float32))

    def halo_field(blocks, picks):
        out = lax.dot_general(
            jnp.stack(blocks), picks, (((2,), (1,)), ((0,), (0,))), precision=HIGH,
            preferred_element_type=jnp.float32,
        )
        return out.reshape(len(halo_dirs) * pad_face, elements)

    faces = mm(select, state).reshape(6, pad_face, 2 * elements)
    kernel_sum = jnp.zeros((pad_nodes, elements), jnp.float32)
    pending = None
    halo_pick_all = None
    for step in range(STEPS):
        high_face, low_face = faces[1], faces[0]
        radial_face = jnp.where(depth_here == 0, faces[5], faces[4])
        if step == 0:
            high_face = with_index(high_face, send_high)
            low_face = with_index(low_face, send_low)
            radial_face = with_index(radial_face, send_radial)
        from_low = from_behind(high_face, "group", 1)
        from_high = from_behind(low_face, "group", -1)
        from_radial = swapped(radial_face, "depth", 0)
        if pending is None:
            state, previous, faces, from_radial = lax.optimization_barrier(
                (state, previous, faces, from_radial)
            )
        else:
            partial, halo, previous, faces, from_radial = lax.optimization_barrier(
                (*pending, previous, faces, from_radial)
            )
            state = partial + mm(into_state, halo)
        if halo_pick_all is None:
            def order_of(x, count):
                return x[index_row, :count].astype(jnp.int32)

            halo_pick_all = jnp.stack(
                [
                    halo_pick(order_of(from_low, elements), elements, face_lists[0]),
                    halo_pick(order_of(from_high, elements), elements, face_lists[1]),
                    halo_pick(order_of(from_radial, radial_count), radial_count, face_lists[4]),
                    halo_pick(order_of(from_radial, radial_count), radial_count, face_lists[5]),
                ]
            )
        grads = mm(grad_op, state).reshape(3, pad_nodes, 2 * elements)
        product = (
            grads[0][:, :elements] * grads[0][:, elements:]
            + grads[1][:, :elements] * grads[1][:, elements:]
            + grads[2][:, :elements] * grads[2][:, elements:]
        )
        kernel_sum = kernel_sum + KERNEL_SCALE * cube * speed_sq * product
        if step == STEPS - 1:
            blocks = lax.dot_general(
                placer,
                kernel_sum[:NODES],
                (((1,), (1,)), ((), ())),
                precision=HIGH,
                preferred_element_type=jnp.float32,
            )
            packed = jnp.concatenate([blocks, labels[:, None]], axis=1)
            packed, grads, faces, previous, state = lax.optimization_barrier(
                (packed, grads, faces, previous, state)
            )
        faces_sw = jnp.stack([faces[f ^ 1] for f in range(6)])
        other = jnp.concatenate(
            [own_part(faces_sw[..., :elements]), own_part(faces_sw[..., elements:])], axis=2
        )
        jumps = PENALTY * square * (faces - other)
        penal = mm(spread, jumps.reshape(6 * pad_face, 2 * elements))
        stiff = mm(stiff_op, (coef * grads).reshape(3 * pad_nodes, 2 * elements))
        partial = 2.0 * state - previous + DT_SQUARED * (-(stiff + penal) / cube)
        partial_faces = mm(select, partial)
        halos = (from_low, from_high, from_radial, from_radial)
        halo = jnp.concatenate(
            [
                halo_field([x[:, :elements] for x in halos], halo_pick_all),
                halo_field([x[:, elements:] for x in halos], halo_pick_all),
            ],
            axis=1,
        )
        faces = (partial_faces + mm(into_faces, halo)).reshape(6, pad_face, 2 * elements)
        previous = state
        pending = (partial, halo)
    state = pending[0] + mm(into_state, pending[1])

    got = lax.all_to_all(packed, ("group", "depth"), 0, 0, tiled=True)
    got_labels = got[:, NODES] - 1.0
    cell_ids = jnp.arange(P_DEV, dtype=jnp.float32)[:, None]
    selector = (got_labels[None, :] == cell_ids).astype(jnp.float32)
    param_grad = mm(selector, got[:, :NODES])
    return (state[:NODES, :elements], state[:NODES, elements:], param_grad)


def solution(mesh):
    return jax.shard_map(
        per_device,
        mesh=mesh,
        in_specs=(
            P(None, ("group", "depth")),
            P(None, ("group", "depth")),
            P(None, ("group", "depth")),
            P(None, ("group", "depth")),
            P(("group", "depth")),
            P(None, ("group", "depth")),
            P(("group", "depth")),
            P(("group", "depth")),
            P(("group", "depth")),
            P(("group", "depth"), None),
            P(("group", "depth")),
        ),
        out_specs=(
            P(None, ("group", "depth")),
            P(None, ("group", "depth")),
            P(("group", "depth"), None),
        ),
        check_vma=False,
    )
```

```python
import math

import jax
import jax.numpy as jnp
import numpy as np
from jax import lax
from jax.sharding import PartitionSpec as P

NODES = 125
STEPS = 4
P_DEV = 128


PENALTY = 40.0
DT_SQUARED = 0.001
KERNEL_SCALE = 0.05
HIGH = lax.Precision.HIGHEST


def from_behind(block, axis, distance):
    devices = range(lax.axis_size(axis))
    route = [((i - distance) % len(devices), i) for i in devices]
    return lax.ppermute(block, axis, route)


def swapped(block, axis, apart):
    count = lax.axis_size(axis)
    route = []
    for low in range(count):
        high = low | 1 << apart
        if high != low and high < count:
            route += [(low, high), (high, low)]
    return lax.ppermute(block, axis, route)


def gll_tables():
    points = np.array([-1.0, -math.sqrt(3.0 / 7.0), 0.0, math.sqrt(3.0 / 7.0), 1.0])
    weights = np.array([0.1, 49.0 / 90.0, 32.0 / 45.0, 49.0 / 90.0, 0.1])
    barycentric = np.array(
        [np.prod([points[i] - points[m] for m in range(5) if m != i]) for i in range(5)]
    )
    derivative = np.zeros((5, 5))
    for i in range(5):
        for j in range(5):
            if i != j:
                derivative[i, j] = barycentric[i] / (barycentric[j] * (points[i] - points[j]))
            else:
                derivative[i, j] = sum((1.0 / (points[i] - points[m]) for m in range(5) if m != i))
    return (weights, derivative)


def node_tables():
    weights, derivative = gll_tables()
    single = np.eye(5)
    operators = [
        np.kron(derivative, np.kron(single, single)),
        np.kron(single, np.kron(derivative, single)),
        np.kron(single, np.kron(single, derivative)),
    ]
    cube = np.kron(weights, np.kron(weights, weights))
    digits = [(n // 25, n // 5 % 5, n % 5) for n in range(125)]
    rows = []
    for f in range(6):
        axis_pick = f // 2
        level = 0 if f % 2 == 0 else 4
        rows.append([n for n in range(125) if digits[n][axis_pick] == level])
    square = np.kron(weights, weights)
    spread = np.zeros((125, 150))
    for f in range(6):
        for a, n in enumerate(rows[f]):
            spread[n, 25 * f + a] = 1.0
    return (operators, cube, rows, square, spread)


def mm(a, b):
    return jnp.dot(a, b, precision=HIGH, preferred_element_type=jnp.float32)


def onehot(rows, index):
    return (jnp.arange(rows, dtype=jnp.int32)[:, None] == index[None, :]).astype(jnp.float32)


def padded_tables(pad_nodes, pad_face):
    operators, cube_np, rows, square_np, spread_np = node_tables()
    grad_op = np.zeros((3 * pad_nodes, pad_nodes))
    stiff_op = np.zeros((pad_nodes, 3 * pad_nodes))
    for d in range(3):
        grad_op[d * pad_nodes : d * pad_nodes + NODES, :NODES] = operators[d]
        stiff_op[:NODES, d * pad_nodes : d * pad_nodes + NODES] = operators[d].T
    select = np.zeros((6 * pad_face, pad_nodes))
    select_swapped = np.zeros((6 * pad_face, pad_nodes))
    for f in range(6):
        for a in range(25):
            select[f * pad_face + a, rows[f][a]] = 1.0
            select_swapped[f * pad_face + a, rows[f ^ 1][a]] = 1.0
    cube = np.ones((pad_nodes, 1))
    cube[:NODES, 0] = cube_np
    square = np.zeros((pad_face, 1))
    square[:25, 0] = square_np
    return grad_op, stiff_op, select, select_swapped, cube, square


def per_device(
    fwd_now,
    fwd_prev,
    adj_now,
    adj_prev,
    speed_sq,
    face_lists,
    send_low,
    send_high,
    send_radial,
    owner_dev,
    param_slot,
):
    pad_nodes, pad_face = 128, 32
    grad_np, stiff_np, select_np, select_sw_np, cube_np, square_np = padded_tables(
        pad_nodes, pad_face
    )
    elements = fwd_now.shape[1]
    groups = lax.axis_size("group")
    layers = lax.axis_size("depth")
    devices = groups * layers
    capacity = elements // devices + elements // (2 * devices) + 2
    radial_count = send_radial.shape[0]
    extra = pad_nodes - NODES

    def padded(a, b):
        return jnp.pad(jnp.concatenate([a, b], axis=1), ((0, extra), (0, 0)))

    state = padded(fwd_now, adj_now)
    previous = padded(fwd_prev, adj_prev)
    depth_here = lax.axis_index("depth")
    grad_op = jnp.asarray(grad_np, jnp.float32)
    stiff_op = jnp.asarray(stiff_np, jnp.float32)
    select = jnp.asarray(select_np, jnp.float32)
    select_swapped = jnp.asarray(select_sw_np, jnp.float32)
    spread = jnp.asarray(select_np.T, jnp.float32)
    cube = jnp.asarray(cube_np, jnp.float32)
    square = jnp.asarray(square_np, jnp.float32)
    speed2 = jnp.concatenate([speed_sq, speed_sq])
    coef = cube * speed2

    own_pick = jnp.stack([onehot(elements, face_lists[f]) for f in range(6)])

    def halo_pick(order, slots, lists):
        return mm(onehot(elements, order), onehot(slots, lists - elements))

    target = owner_dev[:, 0]
    counts = (target[:, None] == jnp.arange(devices, dtype=jnp.int32)[None, :]).astype(jnp.int32)
    before = jnp.cumsum(counts, axis=0) - counts
    position = jnp.sum(before * counts, axis=1)
    placing = target * capacity + position
    placer = onehot(devices * capacity, placing)
    labels = mm(placer, param_slot.astype(jnp.float32) + 1.0)

    def by_field(x, pick):
        return jnp.concatenate([mm(x[:, :elements], pick), mm(x[:, elements:], pick)], axis=1)

    def own_part(x):
        return lax.dot_general(
            x, own_pick, (((2,), (1,)), ((0,), (0,))), precision=HIGH,
            preferred_element_type=jnp.float32,
        )

    halo_dirs = [0, 1, 4, 5]
    spread_halo = np.concatenate(
        [select_np.T[:, f * pad_face : (f + 1) * pad_face] for f in halo_dirs], axis=1
    )
    square_halo = np.tile(square_np[:, 0], len(halo_dirs))
    into_state_np = DT_SQUARED * (spread_halo / cube_np) * (PENALTY * square_halo)[None, :]
    into_state = jnp.asarray(into_state_np, jnp.float32)
    into_faces = jnp.asarray(select_np @ into_state_np, jnp.float32)
    index_row = 25

    def with_index(face, order):
        return face.at[index_row, : order.shape[0]].set(order.astype(jnp.float32))

    def halo_field(blocks, picks):
        out = lax.dot_general(
            jnp.stack(blocks), picks, (((2,), (1,)), ((0,), (0,))), precision=HIGH,
            preferred_element_type=jnp.float32,
        )
        return out.reshape(len(halo_dirs) * pad_face, elements)

    faces = mm(select, state).reshape(6, pad_face, 2 * elements)
    kernel_sum = jnp.zeros((pad_nodes, elements), jnp.float32)
    pending = None
    halo_pick_all = None
    for step in range(STEPS):
        high_face, low_face = faces[1], faces[0]
        radial_face = jnp.where(depth_here == 0, faces[5], faces[4])
        if step == 0:
            high_face = with_index(high_face, send_high)
            low_face = with_index(low_face, send_low)
            radial_face = with_index(radial_face, send_radial)
        from_low = from_behind(high_face, "group", 1)
        from_high = from_behind(low_face, "group", -1)
        from_radial = swapped(radial_face, "depth", 0)
        if pending is None:
            state, previous, faces, from_radial = lax.optimization_barrier(
                (state, previous, faces, from_radial)
            )
        else:
            partial, halo, previous, faces, from_radial = lax.optimization_barrier(
                (*pending, previous, faces, from_radial)
            )
            state = partial + mm(into_state, halo)
        if halo_pick_all is None:
            def order_of(x, count):
                return x[index_row, :count].astype(jnp.int32)

            halo_pick_all = jnp.stack(
                [
                    halo_pick(order_of(from_low, elements), elements, face_lists[0]),
                    halo_pick(order_of(from_high, elements), elements, face_lists[1]),
                    halo_pick(order_of(from_radial, radial_count), radial_count, face_lists[4]),
                    halo_pick(order_of(from_radial, radial_count), radial_count, face_lists[5]),
                ]
            )
        grads = mm(grad_op, state).reshape(3, pad_nodes, 2 * elements)
        product = (
            grads[0][:, :elements] * grads[0][:, elements:]
            + grads[1][:, :elements] * grads[1][:, elements:]
            + grads[2][:, :elements] * grads[2][:, elements:]
        )
        kernel_sum = kernel_sum + KERNEL_SCALE * cube * speed_sq * product
        if step == STEPS - 1:
            blocks = lax.dot_general(
                placer,
                kernel_sum[:NODES],
                (((1,), (1,)), ((), ())),
                precision=HIGH,
                preferred_element_type=jnp.float32,
            )
            packed = jnp.concatenate([blocks, labels[:, None]], axis=1)
            packed, grads, faces, previous, state = lax.optimization_barrier(
                (packed, grads, faces, previous, state)
            )
        faces_sw = jnp.stack([faces[f ^ 1] for f in range(6)])
        other = jnp.concatenate(
            [own_part(faces_sw[..., :elements]), own_part(faces_sw[..., elements:])], axis=2
        )
        jumps = PENALTY * square * (faces - other)
        penal = mm(spread, jumps.reshape(6 * pad_face, 2 * elements))
        stiff = mm(stiff_op, (coef * grads).reshape(3 * pad_nodes, 2 * elements))
        partial = 2.0 * state - previous + DT_SQUARED * (-(stiff + penal) / cube)
        partial_faces = mm(select, partial)
        halos = (from_low, from_high, from_radial, from_radial)
        halo = jnp.concatenate(
            [
                halo_field([x[:, :elements] for x in halos], halo_pick_all),
                halo_field([x[:, elements:] for x in halos], halo_pick_all),
            ],
            axis=1,
        )
        faces = (partial_faces + mm(into_faces, halo)).reshape(6, pad_face, 2 * elements)
        previous = state
        pending = (partial, halo)
    state = pending[0] + mm(into_state, pending[1])

    staged = packed.reshape(groups, layers, capacity, NODES + 1)
    staged = lax.all_to_all(staged, "depth", 1, 1, tiled=True)
    got = lax.all_to_all(staged, "group", 0, 0, tiled=True).reshape(-1, NODES + 1)
    got_labels = got[:, NODES] - 1.0
    cell_ids = jnp.arange(P_DEV, dtype=jnp.float32)[:, None]
    selector = (got_labels[None, :] == cell_ids).astype(jnp.float32)
    param_grad = mm(selector, got[:, :NODES])
    return (state[:NODES, :elements], state[:NODES, elements:], param_grad)


def solution(mesh):
    return jax.shard_map(
        per_device,
        mesh=mesh,
        in_specs=(
            P(None, ("group", "depth")),
            P(None, ("group", "depth")),
            P(None, ("group", "depth")),
            P(None, ("group", "depth")),
            P(("group", "depth")),
            P(None, ("group", "depth")),
            P(("group", "depth")),
            P(("group", "depth")),
            P(("group", "depth")),
            P(("group", "depth"), None),
            P(("group", "depth")),
        ),
        out_specs=(
            P(None, ("group", "depth")),
            P(None, ("group", "depth")),
            P(("group", "depth"), None),
        ),
        check_vma=False,
    )
```

```python
import math

import jax
import jax.numpy as jnp
import numpy as np
from jax import lax
from jax.sharding import PartitionSpec as P

NODES = 125
STEPS = 4
P_DEV = 128


PENALTY = 40.0
DT_SQUARED = 0.001
KERNEL_SCALE = 0.05
HIGH = lax.Precision.HIGHEST


def from_behind(block, axis, distance):
    devices = range(lax.axis_size(axis))
    route = [((i - distance) % len(devices), i) for i in devices]
    return lax.ppermute(block, axis, route)


def swapped(block, axis, apart):
    count = lax.axis_size(axis)
    route = []
    for low in range(count):
        high = low | 1 << apart
        if high != low and high < count:
            route += [(low, high), (high, low)]
    return lax.ppermute(block, axis, route)


def gll_tables():
    points = np.array([-1.0, -math.sqrt(3.0 / 7.0), 0.0, math.sqrt(3.0 / 7.0), 1.0])
    weights = np.array([0.1, 49.0 / 90.0, 32.0 / 45.0, 49.0 / 90.0, 0.1])
    barycentric = np.array(
        [np.prod([points[i] - points[m] for m in range(5) if m != i]) for i in range(5)]
    )
    derivative = np.zeros((5, 5))
    for i in range(5):
        for j in range(5):
            if i != j:
                derivative[i, j] = barycentric[i] / (barycentric[j] * (points[i] - points[j]))
            else:
                derivative[i, j] = sum((1.0 / (points[i] - points[m]) for m in range(5) if m != i))
    return (weights, derivative)


def node_tables():
    weights, derivative = gll_tables()
    single = np.eye(5)
    operators = [
        np.kron(derivative, np.kron(single, single)),
        np.kron(single, np.kron(derivative, single)),
        np.kron(single, np.kron(single, derivative)),
    ]
    cube = np.kron(weights, np.kron(weights, weights))
    digits = [(n // 25, n // 5 % 5, n % 5) for n in range(125)]
    rows = []
    for f in range(6):
        axis_pick = f // 2
        level = 0 if f % 2 == 0 else 4
        rows.append([n for n in range(125) if digits[n][axis_pick] == level])
    square = np.kron(weights, weights)
    spread = np.zeros((125, 150))
    for f in range(6):
        for a, n in enumerate(rows[f]):
            spread[n, 25 * f + a] = 1.0
    return (operators, cube, rows, square, spread)


def mm(a, b):
    return jnp.dot(a, b, precision=HIGH, preferred_element_type=jnp.float32)


def onehot(rows, index):
    return (jnp.arange(rows, dtype=jnp.int32)[:, None] == index[None, :]).astype(jnp.float32)


def padded_tables(pad_nodes, pad_face):
    operators, cube_np, rows, square_np, spread_np = node_tables()
    grad_op = np.zeros((3 * pad_nodes, pad_nodes))
    stiff_op = np.zeros((pad_nodes, 3 * pad_nodes))
    for d in range(3):
        grad_op[d * pad_nodes : d * pad_nodes + NODES, :NODES] = operators[d]
        stiff_op[:NODES, d * pad_nodes : d * pad_nodes + NODES] = operators[d].T
    select = np.zeros((6 * pad_face, pad_nodes))
    select_swapped = np.zeros((6 * pad_face, pad_nodes))
    for f in range(6):
        for a in range(25):
            select[f * pad_face + a, rows[f][a]] = 1.0
            select_swapped[f * pad_face + a, rows[f ^ 1][a]] = 1.0
    cube = np.ones((pad_nodes, 1))
    cube[:NODES, 0] = cube_np
    square = np.zeros((pad_face, 1))
    square[:25, 0] = square_np
    return grad_op, stiff_op, select, select_swapped, cube, square


def per_device(
    fwd_now,
    fwd_prev,
    adj_now,
    adj_prev,
    speed_sq,
    face_lists,
    send_low,
    send_high,
    send_radial,
    owner_dev,
    param_slot,
):
    pad_nodes, pad_face = 128, 32
    grad_np, stiff_np, select_np, select_sw_np, cube_np, square_np = padded_tables(
        pad_nodes, pad_face
    )
    elements = fwd_now.shape[1]
    groups = lax.axis_size("group")
    layers = lax.axis_size("depth")
    devices = groups * layers
    capacity = elements // devices + elements // (2 * devices) + 2
    radial_count = send_radial.shape[0]
    extra = pad_nodes - NODES

    def padded(a, b):
        return jnp.pad(jnp.concatenate([a, b], axis=1), ((0, extra), (0, 0)))

    state = padded(fwd_now, adj_now)
    previous = padded(fwd_prev, adj_prev)
    depth_here = lax.axis_index("depth")
    grad_op = jnp.asarray(grad_np, jnp.float32)
    stiff_op = jnp.asarray(stiff_np, jnp.float32)
    select = jnp.asarray(select_np, jnp.float32)
    select_swapped = jnp.asarray(select_sw_np, jnp.float32)
    spread = jnp.asarray(select_np.T, jnp.float32)
    cube = jnp.asarray(cube_np, jnp.float32)
    square = jnp.asarray(square_np, jnp.float32)
    speed2 = jnp.concatenate([speed_sq, speed_sq])
    coef = cube * speed2

    own_pick = jnp.stack([onehot(elements, face_lists[f]) for f in range(6)])

    def halo_pick(order, slots, lists):
        return mm(onehot(elements, order), onehot(slots, lists - elements))

    target = owner_dev[:, 0]
    counts = (target[:, None] == jnp.arange(devices, dtype=jnp.int32)[None, :]).astype(jnp.int32)
    before = jnp.cumsum(counts, axis=0) - counts
    position = jnp.sum(before * counts, axis=1)
    placing = target * capacity + position
    placer = onehot(devices * capacity, placing)
    labels = mm(placer, param_slot.astype(jnp.float32) + 1.0)

    def by_field(x, pick):
        return jnp.concatenate([mm(x[:, :elements], pick), mm(x[:, elements:], pick)], axis=1)

    def own_part(x):
        return lax.dot_general(
            x, own_pick, (((2,), (1,)), ((0,), (0,))), precision=HIGH,
            preferred_element_type=jnp.float32,
        )

    halo_dirs = [0, 1, 4, 5]
    spread_halo = np.concatenate(
        [select_np.T[:, f * pad_face : (f + 1) * pad_face] for f in halo_dirs], axis=1
    )
    square_halo = np.tile(square_np[:, 0], len(halo_dirs))
    into_state_np = DT_SQUARED * (spread_halo / cube_np) * (PENALTY * square_halo)[None, :]
    into_state = jnp.asarray(into_state_np, jnp.float32)
    into_faces = jnp.asarray(select_np @ into_state_np, jnp.float32)
    index_row = 25

    def with_index(face, order):
        return face.at[index_row, : order.shape[0]].set(order.astype(jnp.float32))

    def halo_field(blocks, picks):
        out = lax.dot_general(
            jnp.stack(blocks), picks, (((2,), (1,)), ((0,), (0,))), precision=HIGH,
            preferred_element_type=jnp.float32,
        )
        return out.reshape(len(halo_dirs) * pad_face, elements)

    faces = mm(select, state).reshape(6, pad_face, 2 * elements)
    kernel_sum = jnp.zeros((pad_nodes, elements), jnp.float32)
    pending = None
    halo_pick_all = None
    for step in range(STEPS):
        last = step == STEPS - 1
        if last:
            state = pending[0] + mm(into_state, pending[1])
            grads = mm(grad_op, state).reshape(3, pad_nodes, 2 * elements)
            product = (
                grads[0][:, :elements] * grads[0][:, elements:]
                + grads[1][:, :elements] * grads[1][:, elements:]
                + grads[2][:, :elements] * grads[2][:, elements:]
            )
            kernel_sum = kernel_sum + KERNEL_SCALE * cube * speed_sq * product
            blocks = lax.dot_general(
                placer,
                kernel_sum[:NODES],
                (((1,), (1,)), ((), ())),
                precision=HIGH,
                preferred_element_type=jnp.float32,
            )
            packed = jnp.concatenate([blocks, labels[:, None]], axis=1)
            packed, faces, state, grads = lax.optimization_barrier((packed, faces, state, grads))
        high_face, low_face = faces[1], faces[0]
        radial_face = jnp.where(depth_here == 0, faces[5], faces[4])
        if step == 0:
            high_face = with_index(high_face, send_high)
            low_face = with_index(low_face, send_low)
            radial_face = with_index(radial_face, send_radial)
        from_low = from_behind(high_face, "group", 1)
        from_high = from_behind(low_face, "group", -1)
        from_radial = swapped(radial_face, "depth", 0)
        if pending is None:
            state, previous, faces, from_radial = lax.optimization_barrier(
                (state, previous, faces, from_radial)
            )
        elif last:
            previous, faces, state, grads, from_radial = lax.optimization_barrier(
                (previous, faces, state, grads, from_radial)
            )
        else:
            partial, halo, previous, faces, from_radial = lax.optimization_barrier(
                (*pending, previous, faces, from_radial)
            )
            state = partial + mm(into_state, halo)
        if halo_pick_all is None:
            def order_of(x, count):
                return x[index_row, :count].astype(jnp.int32)

            halo_pick_all = jnp.stack(
                [
                    halo_pick(order_of(from_low, elements), elements, face_lists[0]),
                    halo_pick(order_of(from_high, elements), elements, face_lists[1]),
                    halo_pick(order_of(from_radial, radial_count), radial_count, face_lists[4]),
                    halo_pick(order_of(from_radial, radial_count), radial_count, face_lists[5]),
                ]
            )
        if not last:
            grads = mm(grad_op, state).reshape(3, pad_nodes, 2 * elements)
            product = (
                grads[0][:, :elements] * grads[0][:, elements:]
                + grads[1][:, :elements] * grads[1][:, elements:]
                + grads[2][:, :elements] * grads[2][:, elements:]
            )
            kernel_sum = kernel_sum + KERNEL_SCALE * cube * speed_sq * product
        faces_sw = jnp.stack([faces[f ^ 1] for f in range(6)])
        other = jnp.concatenate(
            [own_part(faces_sw[..., :elements]), own_part(faces_sw[..., elements:])], axis=2
        )
        jumps = PENALTY * square * (faces - other)
        penal = mm(spread, jumps.reshape(6 * pad_face, 2 * elements))
        stiff = mm(stiff_op, (coef * grads).reshape(3 * pad_nodes, 2 * elements))
        partial = 2.0 * state - previous + DT_SQUARED * (-(stiff + penal) / cube)
        partial_faces = mm(select, partial)
        halos = (from_low, from_high, from_radial, from_radial)
        halo = jnp.concatenate(
            [
                halo_field([x[:, :elements] for x in halos], halo_pick_all),
                halo_field([x[:, elements:] for x in halos], halo_pick_all),
            ],
            axis=1,
        )
        faces = (partial_faces + mm(into_faces, halo)).reshape(6, pad_face, 2 * elements)
        previous = state
        pending = (partial, halo)
    state = pending[0] + mm(into_state, pending[1])

    got = lax.all_to_all(packed, ("group", "depth"), 0, 0, tiled=True)
    got_labels = got[:, NODES] - 1.0
    cell_ids = jnp.arange(P_DEV, dtype=jnp.float32)[:, None]
    selector = (got_labels[None, :] == cell_ids).astype(jnp.float32)
    param_grad = mm(selector, got[:, :NODES])
    return (state[:NODES, :elements], state[:NODES, elements:], param_grad)


def solution(mesh):
    return jax.shard_map(
        per_device,
        mesh=mesh,
        in_specs=(
            P(None, ("group", "depth")),
            P(None, ("group", "depth")),
            P(None, ("group", "depth")),
            P(None, ("group", "depth")),
            P(("group", "depth")),
            P(None, ("group", "depth")),
            P(("group", "depth")),
            P(("group", "depth")),
            P(("group", "depth")),
            P(("group", "depth"), None),
            P(("group", "depth")),
        ),
        out_specs=(
            P(None, ("group", "depth")),
            P(None, ("group", "depth")),
            P(("group", "depth"), None),
        ),
        check_vma=False,
    )
```

```python
import math

import jax
import jax.numpy as jnp
import numpy as np
from jax import lax
from jax.sharding import PartitionSpec as P

NODES = 125
STEPS = 4
P_DEV = 128


PENALTY = 40.0
DT_SQUARED = 0.001
KERNEL_SCALE = 0.05
HIGH = lax.Precision.HIGHEST


def from_behind(block, axis, distance):
    devices = range(lax.axis_size(axis))
    route = [((i - distance) % len(devices), i) for i in devices]
    return lax.ppermute(block, axis, route)


def swapped(block, axis, apart):
    count = lax.axis_size(axis)
    route = []
    for low in range(count):
        high = low | 1 << apart
        if high != low and high < count:
            route += [(low, high), (high, low)]
    return lax.ppermute(block, axis, route)


def gll_tables():
    points = np.array([-1.0, -math.sqrt(3.0 / 7.0), 0.0, math.sqrt(3.0 / 7.0), 1.0])
    weights = np.array([0.1, 49.0 / 90.0, 32.0 / 45.0, 49.0 / 90.0, 0.1])
    barycentric = np.array(
        [np.prod([points[i] - points[m] for m in range(5) if m != i]) for i in range(5)]
    )
    derivative = np.zeros((5, 5))
    for i in range(5):
        for j in range(5):
            if i != j:
                derivative[i, j] = barycentric[i] / (barycentric[j] * (points[i] - points[j]))
            else:
                derivative[i, j] = sum((1.0 / (points[i] - points[m]) for m in range(5) if m != i))
    return (weights, derivative)


def node_tables():
    weights, derivative = gll_tables()
    single = np.eye(5)
    operators = [
        np.kron(derivative, np.kron(single, single)),
        np.kron(single, np.kron(derivative, single)),
        np.kron(single, np.kron(single, derivative)),
    ]
    cube = np.kron(weights, np.kron(weights, weights))
    digits = [(n // 25, n // 5 % 5, n % 5) for n in range(125)]
    rows = []
    for f in range(6):
        axis_pick = f // 2
        level = 0 if f % 2 == 0 else 4
        rows.append([n for n in range(125) if digits[n][axis_pick] == level])
    square = np.kron(weights, weights)
    spread = np.zeros((125, 150))
    for f in range(6):
        for a, n in enumerate(rows[f]):
            spread[n, 25 * f + a] = 1.0
    return (operators, cube, rows, square, spread)


def mm(a, b):
    return jnp.dot(a, b, precision=HIGH, preferred_element_type=jnp.float32)


def onehot(rows, index):
    return (jnp.arange(rows, dtype=jnp.int32)[:, None] == index[None, :]).astype(jnp.float32)


def padded_tables(pad_nodes, pad_face):
    operators, cube_np, rows, square_np, spread_np = node_tables()
    grad_op = np.zeros((3 * pad_nodes, pad_nodes))
    stiff_op = np.zeros((pad_nodes, 3 * pad_nodes))
    for d in range(3):
        grad_op[d * pad_nodes : d * pad_nodes + NODES, :NODES] = operators[d]
        stiff_op[:NODES, d * pad_nodes : d * pad_nodes + NODES] = operators[d].T
    select = np.zeros((6 * pad_face, pad_nodes))
    select_swapped = np.zeros((6 * pad_face, pad_nodes))
    for f in range(6):
        for a in range(25):
            select[f * pad_face + a, rows[f][a]] = 1.0
            select_swapped[f * pad_face + a, rows[f ^ 1][a]] = 1.0
    cube = np.ones((pad_nodes, 1))
    cube[:NODES, 0] = cube_np
    square = np.zeros((pad_face, 1))
    square[:25, 0] = square_np
    return grad_op, stiff_op, select, select_swapped, cube, square


def per_device(
    fwd_now,
    fwd_prev,
    adj_now,
    adj_prev,
    speed_sq,
    face_lists,
    send_low,
    send_high,
    send_radial,
    owner_dev,
    param_slot,
):
    pad_nodes, pad_face = 128, 32
    grad_np, stiff_np, select_np, select_sw_np, cube_np, square_np = padded_tables(
        pad_nodes, pad_face
    )
    elements = fwd_now.shape[1]
    groups = lax.axis_size("group")
    layers = lax.axis_size("depth")
    devices = groups * layers
    capacity = elements // devices + elements // (2 * devices) + 2
    radial_count = send_radial.shape[0]
    extra = pad_nodes - NODES

    def padded(a, b):
        return jnp.pad(jnp.concatenate([a, b], axis=1), ((0, extra), (0, 0)))

    state = padded(fwd_now, adj_now)
    previous = padded(fwd_prev, adj_prev)
    depth_here = lax.axis_index("depth")
    grad_op = jnp.asarray(grad_np, jnp.float32)
    stiff_op = jnp.asarray(stiff_np, jnp.float32)
    select = jnp.asarray(select_np, jnp.float32)
    select_swapped = jnp.asarray(select_sw_np, jnp.float32)
    spread = jnp.asarray(select_np.T, jnp.float32)
    cube = jnp.asarray(cube_np, jnp.float32)
    square = jnp.asarray(square_np, jnp.float32)
    speed2 = jnp.concatenate([speed_sq, speed_sq])
    coef = cube * speed2

    own_pick = jnp.stack([onehot(elements, face_lists[f]) for f in range(6)])

    def halo_pick(order, slots, lists):
        return mm(onehot(elements, order), onehot(slots, lists - elements))

    target = owner_dev[:, 0]
    counts = (target[:, None] == jnp.arange(devices, dtype=jnp.int32)[None, :]).astype(jnp.int32)
    before = jnp.cumsum(counts, axis=0) - counts
    position = jnp.sum(before * counts, axis=1)
    placing = target * capacity + position
    placer = onehot(devices * capacity, placing)
    labels = mm(placer, param_slot.astype(jnp.float32) + 1.0)

    def by_field(x, pick):
        return jnp.concatenate([mm(x[:, :elements], pick), mm(x[:, elements:], pick)], axis=1)

    def own_part(x):
        return lax.dot_general(
            x, own_pick, (((2,), (1,)), ((0,), (0,))), precision=HIGH,
            preferred_element_type=jnp.float32,
        )

    halo_dirs = [0, 1, 4, 5]
    spread_halo = np.concatenate(
        [select_np.T[:, f * pad_face : (f + 1) * pad_face] for f in halo_dirs], axis=1
    )
    square_halo = np.tile(square_np[:, 0], len(halo_dirs))
    into_state_np = DT_SQUARED * (spread_halo / cube_np) * (PENALTY * square_halo)[None, :]
    into_state = jnp.asarray(into_state_np, jnp.float32)
    into_faces = jnp.asarray(select_np @ into_state_np, jnp.float32)
    index_row = 25

    def with_index(face, order):
        return face.at[index_row, : order.shape[0]].set(order.astype(jnp.float32))

    def halo_field(blocks, picks):
        out = lax.dot_general(
            jnp.stack(blocks), picks, (((2,), (1,)), ((0,), (0,))), precision=HIGH,
            preferred_element_type=jnp.float32,
        )
        return out.reshape(len(halo_dirs) * pad_face, elements)

    faces = mm(select, state).reshape(6, pad_face, 2 * elements)
    kernel_sum = jnp.zeros((pad_nodes, elements), jnp.float32)
    pending = None
    halo_pick_all = None
    for step in range(STEPS):
        last = step == STEPS - 1
        if last:
            state = pending[0] + mm(into_state, pending[1])
            grads = mm(grad_op, state).reshape(3, pad_nodes, 2 * elements)
            product = (
                grads[0][:, :elements] * grads[0][:, elements:]
                + grads[1][:, :elements] * grads[1][:, elements:]
                + grads[2][:, :elements] * grads[2][:, elements:]
            )
            kernel_sum = kernel_sum + KERNEL_SCALE * cube * speed_sq * product
            blocks = lax.dot_general(
                placer,
                kernel_sum[:NODES],
                (((1,), (1,)), ((), ())),
                precision=HIGH,
                preferred_element_type=jnp.float32,
            )
            packed = jnp.concatenate([blocks, labels[:, None]], axis=1)
        high_face, low_face = faces[1], faces[0]
        radial_face = jnp.where(depth_here == 0, faces[5], faces[4])
        if step == 0:
            high_face = with_index(high_face, send_high)
            low_face = with_index(low_face, send_low)
            radial_face = with_index(radial_face, send_radial)
        from_low = from_behind(high_face, "group", 1)
        from_high = from_behind(low_face, "group", -1)
        from_radial = swapped(radial_face, "depth", 0)
        if pending is None:
            state, previous, faces, from_radial = lax.optimization_barrier(
                (state, previous, faces, from_radial)
            )
        elif last:
            packed, previous, faces, state, grads, from_radial = lax.optimization_barrier(
                (packed, previous, faces, state, grads, from_radial)
            )
        else:
            partial, halo, previous, faces, from_radial = lax.optimization_barrier(
                (*pending, previous, faces, from_radial)
            )
            state = partial + mm(into_state, halo)
        if halo_pick_all is None:
            def order_of(x, count):
                return x[index_row, :count].astype(jnp.int32)

            halo_pick_all = jnp.stack(
                [
                    halo_pick(order_of(from_low, elements), elements, face_lists[0]),
                    halo_pick(order_of(from_high, elements), elements, face_lists[1]),
                    halo_pick(order_of(from_radial, radial_count), radial_count, face_lists[4]),
                    halo_pick(order_of(from_radial, radial_count), radial_count, face_lists[5]),
                ]
            )
        if not last:
            grads = mm(grad_op, state).reshape(3, pad_nodes, 2 * elements)
            product = (
                grads[0][:, :elements] * grads[0][:, elements:]
                + grads[1][:, :elements] * grads[1][:, elements:]
                + grads[2][:, :elements] * grads[2][:, elements:]
            )
            kernel_sum = kernel_sum + KERNEL_SCALE * cube * speed_sq * product
        faces_sw = jnp.stack([faces[f ^ 1] for f in range(6)])
        other = jnp.concatenate(
            [own_part(faces_sw[..., :elements]), own_part(faces_sw[..., elements:])], axis=2
        )
        jumps = PENALTY * square * (faces - other)
        penal = mm(spread, jumps.reshape(6 * pad_face, 2 * elements))
        stiff = mm(stiff_op, (coef * grads).reshape(3 * pad_nodes, 2 * elements))
        partial = 2.0 * state - previous + DT_SQUARED * (-(stiff + penal) / cube)
        partial_faces = mm(select, partial)
        halos = (from_low, from_high, from_radial, from_radial)
        halo = jnp.concatenate(
            [
                halo_field([x[:, :elements] for x in halos], halo_pick_all),
                halo_field([x[:, elements:] for x in halos], halo_pick_all),
            ],
            axis=1,
        )
        faces = (partial_faces + mm(into_faces, halo)).reshape(6, pad_face, 2 * elements)
        previous = state
        pending = (partial, halo)
    state = pending[0] + mm(into_state, pending[1])

    got = lax.all_to_all(packed, ("group", "depth"), 0, 0, tiled=True)
    got_labels = got[:, NODES] - 1.0
    cell_ids = jnp.arange(P_DEV, dtype=jnp.float32)[:, None]
    selector = (got_labels[None, :] == cell_ids).astype(jnp.float32)
    param_grad = mm(selector, got[:, :NODES])
    return (state[:NODES, :elements], state[:NODES, elements:], param_grad)


def solution(mesh):
    return jax.shard_map(
        per_device,
        mesh=mesh,
        in_specs=(
            P(None, ("group", "depth")),
            P(None, ("group", "depth")),
            P(None, ("group", "depth")),
            P(None, ("group", "depth")),
            P(("group", "depth")),
            P(None, ("group", "depth")),
            P(("group", "depth")),
            P(("group", "depth")),
            P(("group", "depth")),
            P(("group", "depth"), None),
            P(("group", "depth")),
        ),
        out_specs=(
            P(None, ("group", "depth")),
            P(None, ("group", "depth")),
            P(("group", "depth"), None),
        ),
        check_vma=False,
    )
```
